32 devices in a mesh: grp: 4 (over z), ep: 8 (over y, x, core).
Axes of the slice: x: 2, y: 2, z: 4, core: 2. Of those that a mesh axis runs over, the one named last changes fastest.
Arguments:
- resid: bfloat16 [8, 512, 2304], P('ep', 'grp'), may hold values from -6 to 6
- queries: bfloat16 [8, 512, 2304], P('ep', 'grp'), may hold values from -6 to 6
- keys: bfloat16 [8, 512, 2304], P('ep', 'grp'), may hold values from -6 to 6
- values: bfloat16 [8, 512, 2304], P('ep', 'grp'), may hold values from -6 to 6
- tenant: int32 [8, 512], P('ep', 'grp'), may hold values from 0 to 3, never falling along the last dimension, each value on 1 to 256 neighbouring positions
- out_proj: bfloat16 [2304, 2304], replicated, may hold values from -0.125 to 0.125
- norm_gain: float32 [2304], replicated, may hold values from 0.1 to 1.9
- router: bfloat16 [2304, 8], replicated, may hold values from -0.125 to 0.125
- routes: int32 [8, 512, 2], P('ep', 'grp'), may hold values from 0 to 7, all different within a row; in each aligned block of 128 rows (0 to 127, 128 to 255, ..., all dimensions but the last counted through in order) at most 40 rows name the same one
- expert_in: bfloat16 [8, 2304, 2, 5760], P('ep', None, None, 'grp'), as said below
- expert_out: bfloat16 [8, 5760, 2304], P('ep', 'grp'), as said below
Outputs:
- layer_out: bfloat16 [8, 512, 2304], P('ep', 'grp')
The draws below stay inside these ranges and needn't reach their ends.
Inputs may be any that keep to these rules, and one draw needn't show every extreme that they name: Within each sequence tenant ids never fall; one tenant range spans exactly 256 positions. `routes`: the two experts of a token differ; in each aligned block of 128 tokens of one device no expert is named by more than 40 tokens, and some block names some expert exactly 40 times. `expert_in`: entries j and k with j == k // 1 are equal. `expert_out`: entries j and k with j == k // 1 are equal.
All inputs are finite; a program needn't handle non-finite values.
Results may differ from the reference program's by a relative error of at most 0.0056.
Values may be sent and summed in bfloat16 or wider, within the bound.
No kernel may reach another device: no remote copies, remote signals or barrier semaphores. Data moves between devices by JAX's collectives and lax.ppermute only.
A program may use at most 192 MiB of HBM per device.

```python
import math
import jax
import jax.numpy as jnp
import numpy as np
from jax import lax

D = 2304
HEADS = 36
HEAD_DIM = 64
FF = 5760
EXPERTS = 8
TOP = 2
TENANTS = 4
L = 512
SEQS = 8
TOKENS = 4096
REPL = 1
BLOCK = 128
CAP_D = 40
N_GRP = 4
N_EP = 8


def query_key_pair(key):
    shape = (SEQS, L, D)
    first = jax.random.fold_in(key, 71)
    second = jax.random.fold_in(key, 72)
    query_vals = jnp.clip(jax.random.normal(first, shape, jnp.float32), -6.0, 6.0)
    key_vals = jnp.clip(jax.random.normal(second, shape, jnp.float32), -6.0, 6.0)
    return (query_vals, key_vals)


def draw_queries(key, part):
    return query_key_pair(key)[0].astype(jnp.bfloat16)


def draw_keys(key, part):
    return query_key_pair(key)[1].astype(jnp.bfloat16)


def draw_expert_in(key, part):
    base = jnp.clip(jax.random.normal(jax.random.fold_in(key, 81), (EXPERTS, D, 2, FF), jnp.float32), -6.0, 6.0)
    base = base * D ** (-0.5)
    return jnp.repeat(base, REPL, axis=0).astype(jnp.bfloat16)


def draw_expert_out(key, part):
    base = jnp.clip(jax.random.normal(jax.random.fold_in(key, 82), (EXPERTS, FF, D), jnp.float32), -6.0, 6.0)
    base = base * FF ** (-0.5)
    return jnp.repeat(base, REPL, axis=0).astype(jnp.bfloat16)


def levels(stream_key, shape, shards, smallest, top_value):
    gain, own = 1.0, jax.random.fold_in(stream_key, 6)
    for position, shards_of in shards:
        heights = jnp.exp(jax.random.uniform(jax.random.fold_in(own, position), (shards_of,), jnp.float32, smallest / len(shards), top_value / len(shards)))
        gain = gain * jnp.repeat(heights, shape[position] // shards_of).reshape([-1 if axis == position else 1 for axis in range(len(shape))])
    return gain


def length_profile(number_of, total, reach, lean):
    loads = [(1 << 20) // math.isqrt(grade ** lean) + 1 for grade in range(2, number_of + 1)]
    rest, holding = total - reach - (number_of - 1), [1] * (number_of - 1)
    while rest > 0:
        movable = [i for i in range(number_of - 1) if holding[i] < reach]
        mass, remaining = sum([loads[i] for i in movable]), rest
        for i in movable:
            extra = min(reach - holding[i], max(1, remaining * loads[i] // mass), rest)
            holding[i] = holding[i] + extra
            rest = rest - extra
    return np.array([reach] + holding)


def uneven(rng, count, total, bound, skew):
    if count == 2:
        one = jax.random.randint(rng, (), max(1, total - bound), min(bound, total - 1) + 1)
        return jnp.stack([one, total - one])
    tallies = jnp.asarray(length_profile(count, total, bound, skew), jnp.int32)
    couples = (count - 1) // 2
    donor, receiver = tallies[1:1 + 2 * couples:2], tallies[2:2 + 2 * couples:2]
    slack = jnp.minimum(donor - 1, bound - receiver)
    passed = jax.random.randint(jax.random.fold_in(rng, 1), (couples,), 0, 1 << 20) % (slack + 1)
    tallies = tallies.at[1:1 + 2 * couples:2].set(donor - passed).at[2:2 + 2 * couples:2].set(receiver + passed)
    return tallies[jax.random.permutation(jax.random.fold_in(rng, 2), count)]


def assign_block(stream_key, own, number, rows, amount, top, reach, lean):
    order = jax.random.permutation(stream_key, amount)
    heavy_load, usual = load_shares(amount, rows * top, reach, lean, True), load_shares(amount, rows * top, reach, lean, False)
    places = jnp.arange(amount)

    def named(tallies, offset_by):
        used = int((tallies > 0).sum())
        fixed = max(1, used // 4)
        moved = fixed + (places - fixed + offset_by * (used - fixed)) % max(1, amount - fixed)
        return jnp.zeros((amount,), jnp.int32).at[order[jnp.where(places < fixed, places, moved)]].set(jnp.asarray(tallies, jnp.int32))

    tallies = jnp.where(number % 4 == 0, named(heavy_load, number // 4), named(usual, number - number // 4 - 1))
    mixed = jax.random.permutation(jax.random.fold_in(own, 3), amount)
    donor, taker = mixed[0:amount // 2 * 2:2], mixed[1:amount // 2 * 2:2]
    slack = jnp.minimum(tallies[donor] - 1, reach - tallies[taker]) // 2
    slack = jnp.where((donor == order[0]) | (taker == order[0]) | (tallies[taker] == 0), 0, jnp.maximum(slack, 0))
    moved = jax.random.randint(jax.random.fold_in(own, 4), (amount // 2,), 0, 1 << 20) % (slack + 1)
    tallies = tallies.at[donor].add(-moved).at[taker].add(moved)
    labels = jnp.searchsorted(jnp.cumsum(tallies), jnp.arange(rows * top), side="right").astype(jnp.int32)
    listing = labels.reshape(top, rows).T
    listing = listing[jax.random.permutation(jax.random.fold_in(own, 1), rows)]
    offset_by = jax.random.randint(jax.random.fold_in(own, 2), (rows, 1), 0, top)
    return jnp.take_along_axis(listing, (jnp.arange(top)[None, :] + offset_by) % top, axis=1)


def load_shares(count, total, most, skew, full):
    loads = [(1 << 20) // math.isqrt(standing ** skew) + 1 for standing in range(1, count + 1)]
    largest = most if full else min(most, max(-(-total // count), total * loads[0] // sum(loads)))
    least = 1 if total - largest >= count - 1 else 0
    counts, spare = [largest] + [least] * (count - 1), total - largest - least * (count - 1)
    while spare > 0:
        free = [i for i in range(1, count) if counts[i] < largest] or [i for i in range(1, count) if counts[i] < most]
        pool, left = sum([loads[i] for i in free]), spare
        for i in free:
            more = min(most - counts[i], max(1, left * loads[i] // pool), spare)
            counts[i] = counts[i] + more
            spare = spare - more
    return np.array(counts)


def normal_values(own_key, extent, deviation, limit, split=(), dtype=jnp.bfloat16):
    factor_of = levels(own_key, extent, split, -0.22, 0.18) if split else 1.0
    result = jax.random.normal(own_key, extent, jnp.float32) * deviation * factor_of
    return jnp.minimum(jnp.maximum(result, -limit), limit).astype(dtype)


def setup_inputs(seed: int = 0) -> dict:
    seeds = jax.random.split(jax.random.key(seed), 12)
    resid = normal_values(seeds[0], (SEQS, L, D), 1.0, 6.0, ((0, 8), (1, 4)))
    queries = draw_queries(jax.random.fold_in(seeds[11], 71), 0)
    keys = draw_keys(jax.random.fold_in(seeds[11], 71), 0)
    values = normal_values(seeds[3], (SEQS, L, D), 1.0, 6.0, ((0, 8), (1, 4)))
    tenant = jax.vmap(lambda own: jnp.searchsorted(jnp.cumsum(uneven(own, TENANTS, L, L // 2, 0)), jnp.arange(L), side="right"))(jax.random.split(seeds[4], SEQS)).reshape((SEQS, L)).astype(jnp.int32)
    out_proj = normal_values(seeds[5], (D, D), D ** -0.5, 0.125)
    norm_gain = jnp.clip(1.0 + 0.18 * jax.random.normal(seeds[6], (D,), jnp.float32), 0.1, 1.9)
    router = normal_values(seeds[7], (D, EXPERTS), D ** -0.5, 0.125)
    routes_keys = jax.random.split(jax.random.fold_in(seeds[8], 1), SEQS * L // BLOCK)
    routes_turns = jax.random.permutation(jax.random.fold_in(seeds[8], 3), SEQS * L // BLOCK)
    routes = jax.vmap(lambda own, number: assign_block(jax.random.fold_in(seeds[8], 2), own, number, BLOCK, EXPERTS, TOP, CAP_D, 1))(routes_keys, routes_turns).reshape((SEQS, L, TOP))
    expert_in = draw_expert_in(jax.random.fold_in(seeds[11], 71), 0)
    expert_out = draw_expert_out(jax.random.fold_in(seeds[11], 71), 0)
    return dict(resid=resid, queries=queries, keys=keys, values=values, tenant=tenant, out_proj=out_proj, norm_gain=norm_gain, router=router, routes=routes, expert_in=expert_in, expert_out=expert_out)


def attend_one(packed):
    query_rows, key_rows, value_rows, tenant_row = packed
    length = query_rows.shape[0]
    query_heads = query_rows.astype(jnp.float32).reshape(length, HEADS, HEAD_DIM)
    key_heads = key_rows.astype(jnp.float32).reshape(length, HEADS, HEAD_DIM)
    value_heads = value_rows.astype(jnp.float32).reshape(length, HEADS, HEAD_DIM)
    scores = jnp.einsum('qhd,khd->hqk', query_heads, key_heads) * HEAD_DIM ** (-0.5)
    positions = jnp.arange(length).astype(jnp.int32)
    allowed = (positions[:, None] >= positions[None, :]) & (tenant_row[:, None] == tenant_row[None, :])
    scores = jnp.where(allowed[None], scores, -jnp.inf)
    highest = lax.optimization_barrier(jnp.max(scores, axis=-1, keepdims=True))
    probs = jnp.where(allowed[None], jnp.exp(scores - highest), 0.0)
    denominators = lax.optimization_barrier(jnp.sum(probs, axis=-1))
    probs_low = lax.optimization_barrier(probs.astype(jnp.bfloat16))
    weighted = jnp.einsum('hqk,khd->hqd', probs_low.astype(jnp.float32), value_heads)
    mixed = weighted / denominators[..., None]
    return jnp.transpose(mixed, (1, 0, 2)).reshape(length, D).astype(jnp.bfloat16)

def reference(resid, queries, keys, values, tenant, out_proj, norm_gain, router, routes, expert_in, expert_out):
    attention_out = lax.map(attend_one, (queries, keys, values, tenant))
    residual = resid.reshape(TOKENS, D).astype(jnp.float32) + jnp.dot(attention_out.reshape(TOKENS, D), out_proj, preferred_element_type=jnp.float32)
    normed = (residual * lax.rsqrt(lax.optimization_barrier(jnp.mean(residual * residual, axis=-1, keepdims=True)) + 1e-05) * norm_gain).astype(jnp.bfloat16)
    logits = jnp.dot(normed, router, preferred_element_type=jnp.float32)
    chosen = routes.reshape(TOKENS, TOP)
    picked = jnp.take_along_axis(logits, chosen, axis=1)
    gate_weights = jax.nn.softmax(picked, axis=-1).astype(jnp.bfloat16)
    replicas = N_EP // EXPERTS
    weights_in = expert_in[::replicas].reshape(EXPERTS, D, 2 * FF)
    weights_out = expert_out[::replicas]
    route_ids = chosen.reshape(-1)
    order_base = jnp.arange(TOKENS * TOP).astype(jnp.int32)
    route_tokens = (order_base // TOP).astype(jnp.int32)
    route_gates = gate_weights.reshape(-1)
    most_rows = TOKENS // BLOCK * CAP_D
    slices = FF // N_GRP

    def add_expert(total, packed):
        expert_id, w_in, w_out = packed
        sort_key = jnp.where(route_ids == expert_id, 0, TOKENS * TOP).astype(jnp.int32) + order_base
        picked_routes = jnp.argsort(sort_key)[:most_rows].astype(jnp.int32)
        valid = route_ids[picked_routes] == expert_id
        token_ids = route_tokens[picked_routes]
        rows = normed[token_ids]
        both = jnp.dot(rows, w_in, preferred_element_type=jnp.float32)
        hidden = (jax.nn.silu(both[:, :FF]) * both[:, FF:]).astype(jnp.bfloat16)
        partial_value = jnp.einsum('rgf,gfd->grd', hidden.reshape(most_rows, N_GRP, slices).astype(jnp.float32), w_out.reshape(N_GRP, slices, D).astype(jnp.float32))
        partial_low = lax.optimization_barrier(partial_value.astype(jnp.bfloat16))
        expert_output = lax.optimization_barrier(jnp.sum(partial_low.astype(jnp.float32), axis=0)).astype(jnp.bfloat16)
        weight = route_gates[picked_routes].astype(jnp.float32)
        contribution = jnp.where(valid[:, None], expert_output.astype(jnp.float32) * weight[:, None], 0.0)
        return (total.at[token_ids].add(contribution), None)
    moe, _ = lax.scan(add_expert, jnp.zeros((TOKENS, D), jnp.float32), (jnp.arange(EXPERTS).astype(jnp.int32), weights_in, weights_out))
    return (residual + moe).astype(jnp.bfloat16).reshape(SEQS, L, D)
```

```python
import jax
import jax.numpy as jnp
from jax import lax
from jax.sharding import PartitionSpec as P

HEADS = 36
HEAD_DIM = 64
EXPERTS = 8
TOP = 2


NEG = -1e30


def shift_up(x, n_grp):
    return lax.ppermute(x, "grp", perm=[(i, i + 1) for i in range(n_grp - 1)])


def local(
    resid, queries, keys, values, tenant, out_proj, norm_gain, router, routes, expert_in, expert_out
):
    rows_here = resid.shape[1]
    width = resid.shape[2]
    n_ep = lax.axis_size("ep")
    n_grp = lax.axis_size("grp")
    seq_len = rows_here * n_grp
    replicas = n_ep // EXPERTS
    block = rows_here // replicas
    capacity = block * 5 // 16
    me_grp = lax.axis_index("grp")
    offset = me_grp * rows_here
    span = seq_len // 2
    back = min(n_grp - 1, -(-(span - 1) // rows_here))

    query_heads = queries[0].reshape(rows_here, HEADS, HEAD_DIM)
    query_pos = offset + jnp.arange(rows_here, dtype=jnp.int32)
    query_seg = tenant[0]
    scale = HEAD_DIM ** (-0.5)

    key_chunks = [keys[0]]
    value_chunks = [values[0]]
    seg_chunks = [tenant[0]]
    k_cur, v_cur, s_cur = keys[0], values[0], tenant[0]
    for _ in range(back):
        k_cur = shift_up(k_cur, n_grp)
        v_cur = shift_up(v_cur, n_grp)
        s_cur = shift_up(s_cur, n_grp)
        key_chunks.insert(0, k_cur)
        value_chunks.insert(0, v_cur)
        seg_chunks.insert(0, s_cur)
    key_piece = jnp.concatenate(key_chunks, axis=0)
    value_piece = jnp.concatenate(value_chunks, axis=0)
    seg_piece = jnp.concatenate(seg_chunks, axis=0)
    count = key_piece.shape[0]
    key_pos = offset - back * rows_here + jnp.arange(count, dtype=jnp.int32)
    key_heads = key_piece.reshape(count, HEADS, HEAD_DIM)
    value_heads = value_piece.reshape(count, HEADS, HEAD_DIM)
    scores = (
        jnp.einsum("qhd,khd->hqk", query_heads, key_heads, preferred_element_type=jnp.float32)
        * scale
    )
    allowed = (
        (query_pos[:, None] >= key_pos[None, :])
        & (key_pos[None, :] >= 0)
        & (query_seg[:, None] == seg_piece[None, :])
    )
    scores = jnp.where(allowed[None], scores, NEG)
    newest = jnp.max(scores, axis=-1)
    probs = jnp.where(allowed[None], jnp.exp(scores - newest[..., None]), 0.0)
    total = jnp.sum(probs, axis=-1)
    accum = jnp.einsum(
        "hqk,khd->hqd", probs.astype(jnp.bfloat16), value_heads, preferred_element_type=jnp.float32
    )
    attended = (
        jnp.transpose(accum / total[..., None], (1, 0, 2))
        .reshape(rows_here, width)
        .astype(jnp.bfloat16)
    )
    residual = resid[0].astype(jnp.float32) + jnp.dot(
        attended, out_proj, preferred_element_type=jnp.float32
    )
    normed = (
        residual
        * lax.rsqrt(jnp.mean(residual * residual, axis=-1, keepdims=True) + 1e-05)
        * norm_gain
    ).astype(jnp.bfloat16)
    logits = jnp.dot(normed, router, preferred_element_type=jnp.float32)
    local_routes = routes[0]
    expert_ids = jnp.arange(EXPERTS, dtype=jnp.int32)
    picked = jnp.sum(
        jnp.where(local_routes[:, :, None] == expert_ids[None, None, :], logits[:, None, :], 0.0),
        axis=-1,
    )
    gate_weights = jax.nn.softmax(picked, axis=-1).astype(jnp.bfloat16)
    half_id = jnp.arange(rows_here, dtype=jnp.int32) // block
    destination = local_routes * replicas + half_id[:, None]
    flat_dest = destination.reshape(-1)
    onehot = (flat_dest[:, None] == jnp.arange(n_ep, dtype=jnp.int32)[None, :]).astype(jnp.int32)
    earlier = jnp.cumsum(onehot, axis=0) - onehot
    position = jnp.sum(earlier * onehot, axis=1)
    slot = (flat_dest * capacity + position).reshape(rows_here, TOP)
    n_slots = n_ep * capacity
    matches = jnp.arange(n_slots, dtype=jnp.int32)[:, None, None] == slot[None]
    dispatch_table = jnp.any(matches, axis=-1).astype(jnp.bfloat16)
    outgoing = jnp.dot(dispatch_table, normed, preferred_element_type=jnp.float32).astype(
        jnp.bfloat16
    )
    outgoing = outgoing.reshape(n_ep, capacity, width)
    combine = jnp.transpose(
        jnp.sum(jnp.where(matches, gate_weights.astype(jnp.float32)[None], 0.0), axis=-1)
    ).astype(jnp.bfloat16)
    weight_in = expert_in[0]
    weight_out = expert_out[0]
    ff_here = weight_in.shape[2]
    weight_matrix = weight_in.reshape(width, 2 * ff_here)
    in_plane = lax.all_to_all(outgoing, "ep", split_axis=0, concat_axis=0, tiled=True)
    arrived = lax.all_gather(in_plane, "grp", axis=0, tiled=False).reshape(
        n_grp * n_slots, width
    )
    both = jnp.dot(arrived, weight_matrix, preferred_element_type=jnp.float32)
    hidden = (jax.nn.silu(both[:, :ff_here]) * both[:, ff_here:]).astype(jnp.bfloat16)
    partial_value = (
        jnp.dot(hidden, weight_out, preferred_element_type=jnp.float32)
        .astype(jnp.bfloat16)
        .reshape(n_grp, n_ep, capacity, width)
    )
    slices = lax.all_to_all(partial_value, "grp", split_axis=0, concat_axis=0, tiled=True)
    expert_output = jnp.sum(slices.astype(jnp.float32), axis=0).astype(jnp.bfloat16)
    summed = lax.all_to_all(expert_output, "ep", split_axis=0, concat_axis=0, tiled=True).reshape(
        n_slots, width
    )
    moe = jnp.dot(combine, summed, preferred_element_type=jnp.float32)
    return (residual + moe).astype(jnp.bfloat16)[None]


def solution(mesh):
    in_specs = (
        P("ep", "grp", None),
        P("ep", "grp", None),
        P("ep", "grp", None),
        P("ep", "grp", None),
        P("ep", "grp"),
        P(),
        P(),
        P(),
        P("ep", "grp", None),
        P("ep", None, None, "grp"),
        P("ep", "grp", None),
    )
    out_specs = P("ep", "grp", None)
    return jax.shard_map(local, mesh=mesh, in_specs=in_specs, out_specs=out_specs, check_vma=False)
```

```python
import jax
import jax.numpy as jnp
from jax import lax
from jax.sharding import PartitionSpec as P

HEADS = 36
HEAD_DIM = 64
EXPERTS = 8
TOP = 2


NEG = -1e30


def shift_up(x, n_grp):
    return lax.ppermute(x, "grp", perm=[(i, i + 1) for i in range(n_grp - 1)])


def local(
    resid, queries, keys, values, tenant, out_proj, norm_gain, router, routes, expert_in, expert_out
):
    rows_here = resid.shape[1]
    width = resid.shape[2]
    n_ep = lax.axis_size("ep")
    n_grp = lax.axis_size("grp")
    seq_len = rows_here * n_grp
    replicas = n_ep // EXPERTS
    block = rows_here // replicas
    capacity = block * 5 // 16
    me_grp = lax.axis_index("grp")
    offset = me_grp * rows_here
    span = seq_len // 2
    back = min(n_grp - 1, -(-(span - 1) // rows_here))

    query_heads = queries[0].reshape(rows_here, HEADS, HEAD_DIM)
    query_pos = offset + jnp.arange(rows_here, dtype=jnp.int32)
    query_seg = tenant[0]
    scale = HEAD_DIM ** (-0.5)

    key_chunks = [keys[0]]
    value_chunks = [values[0]]
    seg_chunks = [tenant[0]]
    k_cur, v_cur, s_cur = keys[0], values[0], tenant[0]
    for _ in range(back):
        k_cur = shift_up(k_cur, n_grp)
        v_cur = shift_up(v_cur, n_grp)
        s_cur = shift_up(s_cur, n_grp)
        key_chunks.insert(0, k_cur)
        value_chunks.insert(0, v_cur)
        seg_chunks.insert(0, s_cur)
    key_piece = jnp.concatenate(key_chunks, axis=0)
    value_piece = jnp.concatenate(value_chunks, axis=0)
    seg_piece = jnp.concatenate(seg_chunks, axis=0)
    count = key_piece.shape[0]
    key_pos = offset - back * rows_here + jnp.arange(count, dtype=jnp.int32)
    key_heads = key_piece.reshape(count, HEADS, HEAD_DIM)
    value_heads = value_piece.reshape(count, HEADS, HEAD_DIM)
    scores = (
        jnp.einsum("qhd,khd->hqk", query_heads, key_heads, preferred_element_type=jnp.float32)
        * scale
    )
    allowed = (
        (query_pos[:, None] >= key_pos[None, :])
        & (key_pos[None, :] >= 0)
        & (query_seg[:, None] == seg_piece[None, :])
    )
    scores = jnp.where(allowed[None], scores, NEG)
    newest = jnp.max(scores, axis=-1)
    probs = jnp.where(allowed[None], jnp.exp(scores - newest[..., None]), 0.0)
    total = jnp.sum(probs, axis=-1)
    accum = jnp.einsum(
        "hqk,khd->hqd", probs.astype(jnp.bfloat16), value_heads, preferred_element_type=jnp.float32
    )
    attended = (
        jnp.transpose(accum / total[..., None], (1, 0, 2))
        .reshape(rows_here, width)
        .astype(jnp.bfloat16)
    )
    residual = resid[0].astype(jnp.float32) + jnp.dot(
        attended, out_proj, preferred_element_type=jnp.float32
    )
    normed = (
        residual
        * lax.rsqrt(jnp.mean(residual * residual, axis=-1, keepdims=True) + 1e-05)
        * norm_gain
    ).astype(jnp.bfloat16)
    logits = jnp.dot(normed, router, preferred_element_type=jnp.float32)
    local_routes = routes[0]
    expert_ids = jnp.arange(EXPERTS, dtype=jnp.int32)
    picked = jnp.sum(
        jnp.where(local_routes[:, :, None] == expert_ids[None, None, :], logits[:, None, :], 0.0),
        axis=-1,
    )
    gate_weights = jax.nn.softmax(picked, axis=-1).astype(jnp.bfloat16)
    half_id = jnp.arange(rows_here, dtype=jnp.int32) // block
    destination = local_routes * replicas + half_id[:, None]
    flat_dest = destination.reshape(-1)
    onehot = (flat_dest[:, None] == jnp.arange(n_ep, dtype=jnp.int32)[None, :]).astype(jnp.int32)
    earlier = jnp.cumsum(onehot, axis=0) - onehot
    position = jnp.sum(earlier * onehot, axis=1)
    slot = (flat_dest * capacity + position).reshape(rows_here, TOP)
    n_slots = n_ep * capacity
    matches = jnp.arange(n_slots, dtype=jnp.int32)[:, None, None] == slot[None]
    dispatch_table = jnp.any(matches, axis=-1).astype(jnp.bfloat16)
    outgoing = jnp.dot(dispatch_table, normed, preferred_element_type=jnp.float32).astype(
        jnp.bfloat16
    )
    outgoing = outgoing.reshape(n_ep, capacity, width)
    combine = jnp.transpose(
        jnp.sum(jnp.where(matches, gate_weights.astype(jnp.float32)[None], 0.0), axis=-1)
    ).astype(jnp.bfloat16)
    weight_in = expert_in[0]
    weight_out = expert_out[0]
    ff_here = weight_in.shape[2]
    weight_matrix = weight_in.reshape(width, 2 * ff_here)
    in_plane = lax.all_to_all(outgoing, "ep", split_axis=0, concat_axis=0, tiled=True)
    arrived = lax.all_gather(in_plane, "grp", axis=0, tiled=False).reshape(
        n_grp * n_slots, width
    )
    both = jnp.dot(arrived, weight_matrix, preferred_element_type=jnp.float32)
    hidden = (jax.nn.silu(both[:, :ff_here]) * both[:, ff_here:]).astype(jnp.bfloat16)
    partial_value = (
        jnp.dot(hidden, weight_out, preferred_element_type=jnp.float32)
        .astype(jnp.bfloat16)
        .reshape(n_grp, n_ep, capacity, width)
    )
    expert_output = lax.psum_scatter(partial_value, "grp", scatter_dimension=0, tiled=True)[0]
    summed = lax.all_to_all(expert_output, "ep", split_axis=0, concat_axis=0, tiled=True).reshape(
        n_slots, width
    )
    moe = jnp.dot(combine, summed, preferred_element_type=jnp.float32)
    return (residual + moe).astype(jnp.bfloat16)[None]


def solution(mesh):
    in_specs = (
        P("ep", "grp", None),
        P("ep", "grp", None),
        P("ep", "grp", None),
        P("ep", "grp", None),
        P("ep", "grp"),
        P(),
        P(),
        P(),
        P("ep", "grp", None),
        P("ep", None, None, "grp"),
        P("ep", "grp", None),
    )
    out_specs = P("ep", "grp", None)
    return jax.shard_map(local, mesh=mesh, in_specs=in_specs, out_specs=out_specs, check_vma=False)
```

```python
import jax
import jax.numpy as jnp
from jax import lax
from jax.sharding import PartitionSpec as P

HEADS = 36
HEAD_DIM = 64
EXPERTS = 8
TOP = 2


NEG = -1e30


def shift_up(x, n_grp):
    return lax.ppermute(x, "grp", perm=[(i, i + 1) for i in range(n_grp - 1)])


def local(
    resid, queries, keys, values, tenant, out_proj, norm_gain, router, routes, expert_in, expert_out
):
    rows_here = resid.shape[1]
    width = resid.shape[2]
    n_ep = lax.axis_size("ep")
    n_grp = lax.axis_size("grp")
    seq_len = rows_here * n_grp
    replicas = n_ep // EXPERTS
    block = rows_here // replicas
    capacity = block * 5 // 16
    me_grp = lax.axis_index("grp")
    offset = me_grp * rows_here
    span = seq_len // 2
    back = min(n_grp - 1, -(-(span - 1) // rows_here))

    query_heads = queries[0].reshape(rows_here, HEADS, HEAD_DIM)
    query_pos = offset + jnp.arange(rows_here, dtype=jnp.int32)
    query_seg = tenant[0]
    scale = HEAD_DIM ** (-0.5)

    key_chunks = [keys[0]]
    value_chunks = [values[0]]
    seg_chunks = [tenant[0]]
    k_cur, v_cur, s_cur = keys[0], values[0], tenant[0]
    for _ in range(back):
        k_cur = shift_up(k_cur, n_grp)
        v_cur = shift_up(v_cur, n_grp)
        s_cur = shift_up(s_cur, n_grp)
        key_chunks.insert(0, k_cur)
        value_chunks.insert(0, v_cur)
        seg_chunks.insert(0, s_cur)
    key_piece = jnp.concatenate(key_chunks, axis=0)
    value_piece = jnp.concatenate(value_chunks, axis=0)
    seg_piece = jnp.concatenate(seg_chunks, axis=0)
    count = key_piece.shape[0]
    key_pos = offset - back * rows_here + jnp.arange(count, dtype=jnp.int32)
    key_heads = key_piece.reshape(count, HEADS, HEAD_DIM)
    value_heads = value_piece.reshape(count, HEADS, HEAD_DIM)
    scores = (
        jnp.einsum("qhd,khd->hqk", query_heads, key_heads, preferred_element_type=jnp.float32)
        * scale
    )
    allowed = (
        (query_pos[:, None] >= key_pos[None, :])
        & (key_pos[None, :] >= 0)
        & (query_seg[:, None] == seg_piece[None, :])
    )
    scores = jnp.where(allowed[None], scores, NEG)
    newest = jnp.max(scores, axis=-1)
    probs = jnp.where(allowed[None], jnp.exp(scores - newest[..., None]), 0.0)
    total = jnp.sum(probs, axis=-1)
    accum = jnp.einsum(
        "hqk,khd->hqd", probs.astype(jnp.bfloat16), value_heads, preferred_element_type=jnp.float32
    )
    attended = (
        jnp.transpose(accum / total[..., None], (1, 0, 2))
        .reshape(rows_here, width)
        .astype(jnp.bfloat16)
    )
    residual = resid[0].astype(jnp.float32) + jnp.dot(
        attended, out_proj, preferred_element_type=jnp.float32
    )
    normed = (
        residual
        * lax.rsqrt(jnp.mean(residual * residual, axis=-1, keepdims=True) + 1e-05)
        * norm_gain
    ).astype(jnp.bfloat16)
    logits = jnp.dot(normed, router, preferred_element_type=jnp.float32)
    local_routes = routes[0]
    expert_ids = jnp.arange(EXPERTS, dtype=jnp.int32)
    picked = jnp.sum(
        jnp.where(local_routes[:, :, None] == expert_ids[None, None, :], logits[:, None, :], 0.0),
        axis=-1,
    )
    gate_weights = jax.nn.softmax(picked, axis=-1).astype(jnp.bfloat16)
    half_id = jnp.arange(rows_here, dtype=jnp.int32) // block
    destination = local_routes * replicas + half_id[:, None]
    flat_dest = destination.reshape(-1)
    onehot = (flat_dest[:, None] == jnp.arange(n_ep, dtype=jnp.int32)[None, :]).astype(jnp.int32)
    earlier = jnp.cumsum(onehot, axis=0) - onehot
    position = jnp.sum(earlier * onehot, axis=1)
    slot = (flat_dest * capacity + position).reshape(rows_here, TOP)
    n_slots = n_ep * capacity
    matches = jnp.arange(n_slots, dtype=jnp.int32)[:, None, None] == slot[None]
    dispatch_table = jnp.any(matches, axis=-1).astype(jnp.bfloat16)
    outgoing = jnp.dot(dispatch_table, normed, preferred_element_type=jnp.float32).astype(
        jnp.bfloat16
    )
    outgoing = outgoing.reshape(n_ep, capacity, width)
    combine = jnp.transpose(
        jnp.sum(jnp.where(matches, gate_weights.astype(jnp.float32)[None], 0.0), axis=-1)
    ).astype(jnp.bfloat16)
    weight_in = expert_in[0]
    weight_out = expert_out[0]
    ff_here = weight_in.shape[2]
    weight_matrix = weight_in.reshape(width, 2 * ff_here)
    n_chunks = 2 if capacity % 2 == 0 else 1
    per_chunk = capacity // n_chunks
    returned = []
    for c in range(n_chunks):
        piece = outgoing[:, c * per_chunk : (c + 1) * per_chunk]
        in_plane = lax.all_to_all(piece, "ep", split_axis=0, concat_axis=0, tiled=True)
        arrived = lax.all_gather(in_plane, "grp", axis=0, tiled=False).reshape(-1, width)
        both = jnp.dot(arrived, weight_matrix, preferred_element_type=jnp.float32)
        hidden = (jax.nn.silu(both[:, :ff_here]) * both[:, ff_here:]).astype(jnp.bfloat16)
        partial_value = (
            jnp.dot(hidden, weight_out, preferred_element_type=jnp.float32)
            .astype(jnp.bfloat16)
            .reshape(n_grp, n_ep, per_chunk, width)
        )
        expert_output = lax.psum_scatter(partial_value, "grp", scatter_dimension=0, tiled=True)[0]
        returned.append(
            lax.all_to_all(expert_output, "ep", split_axis=0, concat_axis=0, tiled=True)
        )
    summed = jnp.concatenate(returned, axis=1).reshape(n_slots, width)
    moe = jnp.dot(combine, summed, preferred_element_type=jnp.float32)
    return (residual + moe).astype(jnp.bfloat16)[None]


def solution(mesh):
    in_specs = (
        P("ep", "grp", None),
        P("ep", "grp", None),
        P("ep", "grp", None),
        P("ep", "grp", None),
        P("ep", "grp"),
        P(),
        P(),
        P(),
        P("ep", "grp", None),
        P("ep", None, None, "grp"),
        P("ep", "grp", None),
    )
    out_specs = P("ep", "grp", None)
    return jax.shard_map(local, mesh=mesh, in_specs=in_specs, out_specs=out_specs, check_vma=False)
```

```python
import jax
import jax.numpy as jnp
from jax import lax
from jax.sharding import PartitionSpec as P

HEADS = 36
HEAD_DIM = 64
EXPERTS = 8
TOP = 2


NEG = -1e30


def shift_up(x, n_grp):
    return lax.ppermute(x, "grp", perm=[(i, i + 1) for i in range(n_grp - 1)])


def shift_down(x, n_grp):
    return lax.ppermute(x, "grp", perm=[(i + 1, i) for i in range(n_grp - 1)])


def local(
    resid, queries, keys, values, tenant, out_proj, norm_gain, router, routes, expert_in, expert_out
):
    rows_here = resid.shape[1]
    width = resid.shape[2]
    n_ep = lax.axis_size("ep")
    n_grp = lax.axis_size("grp")
    seq_len = rows_here * n_grp
    replicas = n_ep // EXPERTS
    block = rows_here // replicas
    capacity = block * 5 // 16
    me_grp = lax.axis_index("grp")
    offset = me_grp * rows_here
    span = seq_len // 2
    back = min(n_grp - 1, -(-(span - 1) // rows_here))

    query_heads = queries[0].reshape(rows_here, HEADS, HEAD_DIM)
    query_pos = offset + jnp.arange(rows_here, dtype=jnp.int32)
    query_seg = tenant[0]
    scale = HEAD_DIM ** (-0.5)

    key_chunks = [keys[0]]
    value_chunks = [values[0]]
    seg_chunks = [tenant[0]]
    k_cur, v_cur, s_cur = keys[0], values[0], tenant[0]
    for _ in range(back):
        k_cur = shift_up(k_cur, n_grp)
        v_cur = shift_up(v_cur, n_grp)
        s_cur = shift_up(s_cur, n_grp)
        key_chunks.insert(0, k_cur)
        value_chunks.insert(0, v_cur)
        seg_chunks.insert(0, s_cur)
    key_piece = jnp.concatenate(key_chunks, axis=0)
    value_piece = jnp.concatenate(value_chunks, axis=0)
    seg_piece = jnp.concatenate(seg_chunks, axis=0)
    count = key_piece.shape[0]
    key_pos = offset - back * rows_here + jnp.arange(count, dtype=jnp.int32)
    key_heads = key_piece.reshape(count, HEADS, HEAD_DIM)
    value_heads = value_piece.reshape(count, HEADS, HEAD_DIM)
    scores = (
        jnp.einsum("qhd,khd->hqk", query_heads, key_heads, preferred_element_type=jnp.float32)
        * scale
    )
    allowed = (
        (query_pos[:, None] >= key_pos[None, :])
        & (key_pos[None, :] >= 0)
        & (query_seg[:, None] == seg_piece[None, :])
    )
    scores = jnp.where(allowed[None], scores, NEG)
    newest = jnp.max(scores, axis=-1)
    probs = jnp.where(allowed[None], jnp.exp(scores - newest[..., None]), 0.0)
    total = jnp.sum(probs, axis=-1)
    accum = jnp.einsum(
        "hqk,khd->hqd", probs.astype(jnp.bfloat16), value_heads, preferred_element_type=jnp.float32
    )
    attended = (
        jnp.transpose(accum / total[..., None], (1, 0, 2))
        .reshape(rows_here, width)
        .astype(jnp.bfloat16)
    )
    residual = resid[0].astype(jnp.float32) + jnp.dot(
        attended, out_proj, preferred_element_type=jnp.float32
    )
    normed = (
        residual
        * lax.rsqrt(jnp.mean(residual * residual, axis=-1, keepdims=True) + 1e-05)
        * norm_gain
    ).astype(jnp.bfloat16)
    logits = jnp.dot(normed, router, preferred_element_type=jnp.float32)
    local_routes = routes[0]
    expert_ids = jnp.arange(EXPERTS, dtype=jnp.int32)
    picked = jnp.sum(
        jnp.where(local_routes[:, :, None] == expert_ids[None, None, :], logits[:, None, :], 0.0),
        axis=-1,
    )
    gate_weights = jax.nn.softmax(picked, axis=-1).astype(jnp.bfloat16)
    half_id = jnp.arange(rows_here, dtype=jnp.int32) // block
    destination = local_routes * replicas + half_id[:, None]
    flat_dest = destination.reshape(-1)
    onehot = (flat_dest[:, None] == jnp.arange(n_ep, dtype=jnp.int32)[None, :]).astype(jnp.int32)
    earlier = jnp.cumsum(onehot, axis=0) - onehot
    position = jnp.sum(earlier * onehot, axis=1)
    slot = (flat_dest * capacity + position).reshape(rows_here, TOP)
    n_slots = n_ep * capacity
    matches = jnp.arange(n_slots, dtype=jnp.int32)[:, None, None] == slot[None]
    dispatch_table = jnp.any(matches, axis=-1).astype(jnp.bfloat16)
    outgoing = jnp.dot(dispatch_table, normed, preferred_element_type=jnp.float32).astype(
        jnp.bfloat16
    )
    outgoing = outgoing.reshape(n_ep, capacity, width)
    combine = jnp.transpose(
        jnp.sum(jnp.where(matches, gate_weights.astype(jnp.float32)[None], 0.0), axis=-1)
    ).astype(jnp.bfloat16)
    weight_in = expert_in[0]
    weight_out = expert_out[0]
    ff_here = weight_in.shape[2]
    weight_matrix = weight_in.reshape(width, 2 * ff_here)
    def expert(rows):
        both = jnp.dot(rows, weight_matrix, preferred_element_type=jnp.float32)
        hidden = (jax.nn.silu(both[:, :ff_here]) * both[:, ff_here:]).astype(jnp.bfloat16)
        return jnp.dot(hidden, weight_out, preferred_element_type=jnp.float32).astype(jnp.bfloat16)

    own = lax.all_to_all(outgoing, "ep", split_axis=0, concat_axis=0, tiled=True).reshape(
        n_slots, width
    )
    partial_own = expert(own)
    from_below, from_above = [None] * n_grp, [None] * n_grp
    up_rows, down_rows = own, own
    for r in range(1, n_grp):
        up_rows = shift_up(up_rows, n_grp)
        down_rows = shift_down(down_rows, n_grp)
        if 2 * r <= n_grp - 1:
            from_below[r] = expert(up_rows)
            from_above[r] = expert(down_rows)
        else:
            chosen = jnp.where(me_grp >= r, up_rows, down_rows)
            from_below[r] = from_above[r] = expert(chosen)
    up_sum = down_sum = None
    for r in range(1, n_grp):
        send_up = from_above[n_grp - r]
        send_down = from_below[n_grp - r]
        if r > 1:
            send_up = (send_up.astype(jnp.float32) + up_sum.astype(jnp.float32)).astype(
                jnp.bfloat16
            )
            send_down = (send_down.astype(jnp.float32) + down_sum.astype(jnp.float32)).astype(
                jnp.bfloat16
            )
        up_sum = shift_up(send_up, n_grp)
        down_sum = shift_down(send_down, n_grp)
    expert_output = (
        partial_own.astype(jnp.float32) + up_sum.astype(jnp.float32) + down_sum.astype(jnp.float32)
    ).astype(jnp.bfloat16)
    summed = lax.all_to_all(
        expert_output.reshape(n_ep, capacity, width), "ep", split_axis=0, concat_axis=0, tiled=True
    ).reshape(n_slots, width)
    moe = jnp.dot(combine, summed, preferred_element_type=jnp.float32)
    return (residual + moe).astype(jnp.bfloat16)[None]


def solution(mesh):
    in_specs = (
        P("ep", "grp", None),
        P("ep", "grp", None),
        P("ep", "grp", None),
        P("ep", "grp", None),
        P("ep", "grp"),
        P(),
        P(),
        P(),
        P("ep", "grp", None),
        P("ep", None, None, "grp"),
        P("ep", "grp", None),
    )
    out_specs = P("ep", "grp", None)
    return jax.shard_map(local, mesh=mesh, in_specs=in_specs, out_specs=out_specs, check_vma=False)
```

```python
import jax
import jax.numpy as jnp
from jax import lax
from jax.sharding import PartitionSpec as P

HEADS = 36
HEAD_DIM = 64
EXPERTS = 8
TOP = 2


NEG = -1e30


def shift_up(x, n_grp):
    return lax.ppermute(x, "grp", perm=[(i, i + 1) for i in range(n_grp - 1)])


def shift_down(x, n_grp):
    return lax.ppermute(x, "grp", perm=[(i + 1, i) for i in range(n_grp - 1)])


def local(
    resid, queries, keys, values, tenant, out_proj, norm_gain, router, routes, expert_in, expert_out
):
    rows_here = resid.shape[1]
    width = resid.shape[2]
    n_ep = lax.axis_size("ep")
    n_grp = lax.axis_size("grp")
    seq_len = rows_here * n_grp
    replicas = n_ep // EXPERTS
    block = rows_here // replicas
    capacity = block * 5 // 16
    me_grp = lax.axis_index("grp")
    offset = me_grp * rows_here
    span = seq_len // 2
    back = min(n_grp - 1, -(-(span - 1) // rows_here))

    query_heads = queries[0].reshape(rows_here, HEADS, HEAD_DIM)
    query_pos = offset + jnp.arange(rows_here, dtype=jnp.int32)
    query_seg = tenant[0]
    scale = HEAD_DIM ** (-0.5)

    key_chunks = [keys[0]]
    value_chunks = [values[0]]
    seg_chunks = [tenant[0]]
    k_cur, v_cur, s_cur = keys[0], values[0], tenant[0]
    for _ in range(back):
        k_cur = shift_up(k_cur, n_grp)
        v_cur = shift_up(v_cur, n_grp)
        s_cur = shift_up(s_cur, n_grp)
        key_chunks.insert(0, k_cur)
        value_chunks.insert(0, v_cur)
        seg_chunks.insert(0, s_cur)
    key_piece = jnp.concatenate(key_chunks, axis=0)
    value_piece = jnp.concatenate(value_chunks, axis=0)
    seg_piece = jnp.concatenate(seg_chunks, axis=0)
    count = key_piece.shape[0]
    key_pos = offset - back * rows_here + jnp.arange(count, dtype=jnp.int32)
    key_heads = key_piece.reshape(count, HEADS, HEAD_DIM)
    value_heads = value_piece.reshape(count, HEADS, HEAD_DIM)
    scores = (
        jnp.einsum("qhd,khd->hqk", query_heads, key_heads, preferred_element_type=jnp.float32)
        * scale
    )
    allowed = (
        (query_pos[:, None] >= key_pos[None, :])
        & (key_pos[None, :] >= 0)
        & (query_seg[:, None] == seg_piece[None, :])
    )
    scores = jnp.where(allowed[None], scores, NEG)
    newest = jnp.max(scores, axis=-1)
    probs = jnp.where(allowed[None], jnp.exp(scores - newest[..., None]), 0.0)
    total = jnp.sum(probs, axis=-1)
    accum = jnp.einsum(
        "hqk,khd->hqd", probs.astype(jnp.bfloat16), value_heads, preferred_element_type=jnp.float32
    )
    attended = (
        jnp.transpose(accum / total[..., None], (1, 0, 2))
        .reshape(rows_here, width)
        .astype(jnp.bfloat16)
    )
    residual = resid[0].astype(jnp.float32) + jnp.dot(
        attended, out_proj, preferred_element_type=jnp.float32
    )
    normed = (
        residual
        * lax.rsqrt(jnp.mean(residual * residual, axis=-1, keepdims=True) + 1e-05)
        * norm_gain
    ).astype(jnp.bfloat16)
    logits = jnp.dot(normed, router, preferred_element_type=jnp.float32)
    local_routes = routes[0]
    expert_ids = jnp.arange(EXPERTS, dtype=jnp.int32)
    picked = jnp.sum(
        jnp.where(local_routes[:, :, None] == expert_ids[None, None, :], logits[:, None, :], 0.0),
        axis=-1,
    )
    gate_weights = jax.nn.softmax(picked, axis=-1).astype(jnp.bfloat16)
    half_id = jnp.arange(rows_here, dtype=jnp.int32) // block
    destination = local_routes * replicas + half_id[:, None]
    flat_dest = destination.reshape(-1)
    onehot = (flat_dest[:, None] == jnp.arange(n_ep, dtype=jnp.int32)[None, :]).astype(jnp.int32)
    earlier = jnp.cumsum(onehot, axis=0) - onehot
    position = jnp.sum(earlier * onehot, axis=1)
    slot = (flat_dest * capacity + position).reshape(rows_here, TOP)
    n_slots = n_ep * capacity
    matches = jnp.arange(n_slots, dtype=jnp.int32)[:, None, None] == slot[None]
    dispatch_table = jnp.any(matches, axis=-1).astype(jnp.bfloat16)
    outgoing = jnp.dot(dispatch_table, normed, preferred_element_type=jnp.float32).astype(
        jnp.bfloat16
    )
    outgoing = outgoing.reshape(n_ep, capacity, width)
    combine = jnp.transpose(
        jnp.sum(jnp.where(matches, gate_weights.astype(jnp.float32)[None], 0.0), axis=-1)
    ).astype(jnp.bfloat16)
    weight_in = expert_in[0]
    weight_out = expert_out[0]
    ff_here = weight_in.shape[2]
    weight_matrix = weight_in.reshape(width, 2 * ff_here)
    def expert(rows):
        both = jnp.dot(rows, weight_matrix, preferred_element_type=jnp.float32)
        hidden = (jax.nn.silu(both[:, :ff_here]) * both[:, ff_here:]).astype(jnp.bfloat16)
        return jnp.dot(hidden, weight_out, preferred_element_type=jnp.float32).astype(jnp.bfloat16)

    own = lax.all_to_all(outgoing, "ep", split_axis=0, concat_axis=0, tiled=True).reshape(
        n_slots, width
    )
    partial_own = expert(own)
    from_below, from_above = [None] * n_grp, [None] * n_grp
    up_rows, down_rows = own, own
    pending = []
    for r in range(1, n_grp):
        up_rows, down_rows, _ = lax.optimization_barrier((up_rows, down_rows, pending))
        pending = [partial_own] if r == 1 else [from_below[r - 1], from_above[r - 1]]
        up_rows = shift_up(up_rows, n_grp)
        down_rows = shift_down(down_rows, n_grp)
        if 2 * r <= n_grp - 1:
            from_below[r] = expert(up_rows)
            from_above[r] = expert(down_rows)
        else:
            chosen = jnp.where(me_grp >= r, up_rows, down_rows)
            from_below[r] = from_above[r] = expert(chosen)
    up_sum = down_sum = None
    for r in range(1, n_grp):
        send_up = from_above[n_grp - r]
        send_down = from_below[n_grp - r]
        if r == 1:
            send_up, send_down, _ = lax.optimization_barrier((send_up, send_down, pending))
        if r > 1:
            send_up = (send_up.astype(jnp.float32) + up_sum.astype(jnp.float32)).astype(
                jnp.bfloat16
            )
            send_down = (send_down.astype(jnp.float32) + down_sum.astype(jnp.float32)).astype(
                jnp.bfloat16
            )
        up_sum = shift_up(send_up, n_grp)
        down_sum = shift_down(send_down, n_grp)
    expert_output = (
        partial_own.astype(jnp.float32) + up_sum.astype(jnp.float32) + down_sum.astype(jnp.float32)
    ).astype(jnp.bfloat16)
    summed = lax.all_to_all(
        expert_output.reshape(n_ep, capacity, width), "ep", split_axis=0, concat_axis=0, tiled=True
    ).reshape(n_slots, width)
    moe = jnp.dot(combine, summed, preferred_element_type=jnp.float32)
    return (residual + moe).astype(jnp.bfloat16)[None]


def solution(mesh):
    in_specs = (
        P("ep", "grp", None),
        P("ep", "grp", None),
        P("ep", "grp", None),
        P("ep", "grp", None),
        P("ep", "grp"),
        P(),
        P(),
        P(),
        P("ep", "grp", None),
        P("ep", None, None, "grp"),
        P("ep", "grp", None),
    )
    out_specs = P("ep", "grp", None)
    return jax.shard_map(local, mesh=mesh, in_specs=in_specs, out_specs=out_specs, check_vma=False)
```

```python
import jax
import jax.numpy as jnp
from jax import lax
from jax.sharding import PartitionSpec as P

HEADS = 36
HEAD_DIM = 64
EXPERTS = 8
TOP = 2


NEG = -1e30


def shift_up(x, first, last):
    return lax.ppermute(x, "grp", perm=[(i, i + 1) for i in range(first, last + 1)])


def shift_down(x, first, last):
    return lax.ppermute(x, "grp", perm=[(i, i - 1) for i in range(first, last + 1)])


def local(
    resid, queries, keys, values, tenant, out_proj, norm_gain, router, routes, expert_in, expert_out
):
    rows_here = resid.shape[1]
    width = resid.shape[2]
    n_ep = lax.axis_size("ep")
    n_grp = lax.axis_size("grp")
    seq_len = rows_here * n_grp
    replicas = n_ep // EXPERTS
    block = rows_here // replicas
    capacity = block * 5 // 16
    me_grp = lax.axis_index("grp")
    offset = me_grp * rows_here
    span = seq_len // 2
    back = min(n_grp - 1, -(-(span - 1) // rows_here))

    query_heads = queries[0].reshape(rows_here, HEADS, HEAD_DIM)
    query_pos = offset + jnp.arange(rows_here, dtype=jnp.int32)
    query_seg = tenant[0]
    scale = HEAD_DIM ** (-0.5)

    key_chunks = [keys[0]]
    value_chunks = [values[0]]
    seg_chunks = [tenant[0]]
    k_cur, v_cur, s_cur = keys[0], values[0], tenant[0]
    for _ in range(back):
        k_cur = shift_up(k_cur, 0, n_grp - 2)
        v_cur = shift_up(v_cur, 0, n_grp - 2)
        s_cur = shift_up(s_cur, 0, n_grp - 2)
        key_chunks.insert(0, k_cur)
        value_chunks.insert(0, v_cur)
        seg_chunks.insert(0, s_cur)
    key_piece = jnp.concatenate(key_chunks, axis=0)
    value_piece = jnp.concatenate(value_chunks, axis=0)
    seg_piece = jnp.concatenate(seg_chunks, axis=0)
    count = key_piece.shape[0]
    key_pos = offset - back * rows_here + jnp.arange(count, dtype=jnp.int32)
    key_heads = key_piece.reshape(count, HEADS, HEAD_DIM)
    value_heads = value_piece.reshape(count, HEADS, HEAD_DIM)
    scores = (
        jnp.einsum("qhd,khd->hqk", query_heads, key_heads, preferred_element_type=jnp.float32)
        * scale
    )
    allowed = (
        (query_pos[:, None] >= key_pos[None, :])
        & (key_pos[None, :] >= 0)
        & (query_seg[:, None] == seg_piece[None, :])
    )
    scores = jnp.where(allowed[None], scores, NEG)
    newest = jnp.max(scores, axis=-1)
    probs = jnp.where(allowed[None], jnp.exp(scores - newest[..., None]), 0.0)
    total = jnp.sum(probs, axis=-1)
    accum = jnp.einsum(
        "hqk,khd->hqd", probs.astype(jnp.bfloat16), value_heads, preferred_element_type=jnp.float32
    )
    attended = (
        jnp.transpose(accum / total[..., None], (1, 0, 2))
        .reshape(rows_here, width)
        .astype(jnp.bfloat16)
    )
    residual = resid[0].astype(jnp.float32) + jnp.dot(
        attended, out_proj, preferred_element_type=jnp.float32
    )
    normed = (
        residual
        * lax.rsqrt(jnp.mean(residual * residual, axis=-1, keepdims=True) + 1e-05)
        * norm_gain
    ).astype(jnp.bfloat16)
    logits = jnp.dot(normed, router, preferred_element_type=jnp.float32)
    local_routes = routes[0]
    expert_ids = jnp.arange(EXPERTS, dtype=jnp.int32)
    picked = jnp.sum(
        jnp.where(local_routes[:, :, None] == expert_ids[None, None, :], logits[:, None, :], 0.0),
        axis=-1,
    )
    gate_weights = jax.nn.softmax(picked, axis=-1).astype(jnp.bfloat16)
    half_id = jnp.arange(rows_here, dtype=jnp.int32) // block
    destination = local_routes * replicas + half_id[:, None]
    flat_dest = destination.reshape(-1)
    onehot = (flat_dest[:, None] == jnp.arange(n_ep, dtype=jnp.int32)[None, :]).astype(jnp.int32)
    earlier = jnp.cumsum(onehot, axis=0) - onehot
    position = jnp.sum(earlier * onehot, axis=1)
    slot = (flat_dest * capacity + position).reshape(rows_here, TOP)
    n_slots = n_ep * capacity
    matches = jnp.arange(n_slots, dtype=jnp.int32)[:, None, None] == slot[None]
    dispatch_table = jnp.any(matches, axis=-1).astype(jnp.bfloat16)
    outgoing = jnp.dot(dispatch_table, normed, preferred_element_type=jnp.float32).astype(
        jnp.bfloat16
    )
    outgoing = outgoing.reshape(n_ep, capacity, width)
    combine = jnp.transpose(
        jnp.sum(jnp.where(matches, gate_weights.astype(jnp.float32)[None], 0.0), axis=-1)
    ).astype(jnp.bfloat16)
    weight_in = expert_in[0]
    weight_out = expert_out[0]
    ff_here = weight_in.shape[2]
    weight_matrix = weight_in.reshape(width, 2 * ff_here)
    def expert(rows):
        both = jnp.dot(rows, weight_matrix, preferred_element_type=jnp.float32)
        hidden = (jax.nn.silu(both[:, :ff_here]) * both[:, ff_here:]).astype(jnp.bfloat16)
        return jnp.dot(hidden, weight_out, preferred_element_type=jnp.float32).astype(jnp.bfloat16)

    own = lax.all_to_all(outgoing, "ep", split_axis=0, concat_axis=0, tiled=True).reshape(
        n_slots, width
    )
    partial_own = expert(own)
    from_below, from_above = [None] * n_grp, [None] * n_grp
    up_rows, down_rows = own, own
    pending = []
    for r in range(1, n_grp):
        up_rows, down_rows, _ = lax.optimization_barrier((up_rows, down_rows, pending))
        pending = [partial_own] if r == 1 else [from_below[r - 1], from_above[r - 1]]
        up_rows = shift_up(up_rows, r - 1, n_grp - 2)
        down_rows = shift_down(down_rows, 1, n_grp - r)
        if 2 * r <= n_grp - 1:
            pair = expert(jnp.concatenate([up_rows, down_rows], axis=0))
            from_below[r], from_above[r] = pair[:n_slots], pair[n_slots:]
        else:
            chosen = jnp.where(me_grp >= r, up_rows, down_rows)
            from_below[r] = from_above[r] = expert(chosen)
    up_sum = down_sum = None
    for r in range(1, n_grp):
        send_up = from_above[n_grp - r]
        send_down = from_below[n_grp - r]
        if r == 1:
            send_up, send_down, _ = lax.optimization_barrier((send_up, send_down, pending))
        if r > 1:
            send_up = (send_up.astype(jnp.float32) + up_sum.astype(jnp.float32)).astype(
                jnp.bfloat16
            )
            send_down = (send_down.astype(jnp.float32) + down_sum.astype(jnp.float32)).astype(
                jnp.bfloat16
            )
        up_sum = shift_up(send_up, 0, r - 1)
        down_sum = shift_down(send_down, n_grp - r, n_grp - 1)
    expert_output = (
        partial_own.astype(jnp.float32) + up_sum.astype(jnp.float32) + down_sum.astype(jnp.float32)
    ).astype(jnp.bfloat16)
    summed = lax.all_to_all(
        expert_output.reshape(n_ep, capacity, width), "ep", split_axis=0, concat_axis=0, tiled=True
    ).reshape(n_slots, width)
    moe = jnp.dot(combine, summed, preferred_element_type=jnp.float32)
    return (residual + moe).astype(jnp.bfloat16)[None]


def solution(mesh):
    in_specs = (
        P("ep", "grp", None),
        P("ep", "grp", None),
        P("ep", "grp", None),
        P("ep", "grp", None),
        P("ep", "grp"),
        P(),
        P(),
        P(),
        P("ep", "grp", None),
        P("ep", None, None, "grp"),
        P("ep", "grp", None),
    )
    out_specs = P("ep", "grp", None)
    return jax.shard_map(local, mesh=mesh, in_specs=in_specs, out_specs=out_specs, check_vma=False)
```

```python
import jax
import jax.numpy as jnp
from jax import lax
from jax.sharding import PartitionSpec as P

HEADS = 36
HEAD_DIM = 64
EXPERTS = 8
TOP = 2


NEG = -1e30


def shift_up(x, first, last):
    return lax.ppermute(x, "grp", perm=[(i, i + 1) for i in range(first, last + 1)])


def shift_down(x, first, last):
    return lax.ppermute(x, "grp", perm=[(i, i - 1) for i in range(first, last + 1)])


def after(pending, x):
    for p in pending:
        x = x + (p[0, 0] * 0).astype(x.dtype)
    return x


def local(
    resid, queries, keys, values, tenant, out_proj, norm_gain, router, routes, expert_in, expert_out
):
    rows_here = resid.shape[1]
    width = resid.shape[2]
    n_ep = lax.axis_size("ep")
    n_grp = lax.axis_size("grp")
    seq_len = rows_here * n_grp
    replicas = n_ep // EXPERTS
    block = rows_here // replicas
    capacity = block * 5 // 16
    me_grp = lax.axis_index("grp")
    offset = me_grp * rows_here
    span = seq_len // 2
    back = min(n_grp - 1, -(-(span - 1) // rows_here))

    query_heads = queries[0].reshape(rows_here, HEADS, HEAD_DIM)
    query_pos = offset + jnp.arange(rows_here, dtype=jnp.int32)
    query_seg = tenant[0]
    scale = HEAD_DIM ** (-0.5)

    key_chunks = [keys[0]]
    value_chunks = [values[0]]
    seg_chunks = [tenant[0]]
    k_cur, v_cur, s_cur = keys[0], values[0], tenant[0]
    for _ in range(back):
        k_cur = shift_up(k_cur, 0, n_grp - 2)
        v_cur = shift_up(v_cur, 0, n_grp - 2)
        s_cur = shift_up(s_cur, 0, n_grp - 2)
        key_chunks.insert(0, k_cur)
        value_chunks.insert(0, v_cur)
        seg_chunks.insert(0, s_cur)
    key_piece = jnp.concatenate(key_chunks, axis=0)
    value_piece = jnp.concatenate(value_chunks, axis=0)
    seg_piece = jnp.concatenate(seg_chunks, axis=0)
    count = key_piece.shape[0]
    key_pos = offset - back * rows_here + jnp.arange(count, dtype=jnp.int32)
    key_heads = key_piece.reshape(count, HEADS, HEAD_DIM)
    value_heads = value_piece.reshape(count, HEADS, HEAD_DIM)
    scores = (
        jnp.einsum("qhd,khd->hqk", query_heads, key_heads, preferred_element_type=jnp.float32)
        * scale
    )
    allowed = (
        (query_pos[:, None] >= key_pos[None, :])
        & (key_pos[None, :] >= 0)
        & (query_seg[:, None] == seg_piece[None, :])
    )
    scores = jnp.where(allowed[None], scores, NEG)
    newest = jnp.max(scores, axis=-1)
    probs = jnp.where(allowed[None], jnp.exp(scores - newest[..., None]), 0.0)
    total = jnp.sum(probs, axis=-1)
    accum = jnp.einsum(
        "hqk,khd->hqd", probs.astype(jnp.bfloat16), value_heads, preferred_element_type=jnp.float32
    )
    attended = (
        jnp.transpose(accum / total[..., None], (1, 0, 2))
        .reshape(rows_here, width)
        .astype(jnp.bfloat16)
    )
    residual = resid[0].astype(jnp.float32) + jnp.dot(
        attended, out_proj, preferred_element_type=jnp.float32
    )
    normed = (
        residual
        * lax.rsqrt(jnp.mean(residual * residual, axis=-1, keepdims=True) + 1e-05)
        * norm_gain
    ).astype(jnp.bfloat16)
    logits = jnp.dot(normed, router, preferred_element_type=jnp.float32)
    local_routes = routes[0]
    expert_ids = jnp.arange(EXPERTS, dtype=jnp.int32)
    picked = jnp.sum(
        jnp.where(local_routes[:, :, None] == expert_ids[None, None, :], logits[:, None, :], 0.0),
        axis=-1,
    )
    gate_weights = jax.nn.softmax(picked, axis=-1).astype(jnp.bfloat16)
    half_id = jnp.arange(rows_here, dtype=jnp.int32) // block
    destination = local_routes * replicas + half_id[:, None]
    flat_dest = destination.reshape(-1)
    onehot = (flat_dest[:, None] == jnp.arange(n_ep, dtype=jnp.int32)[None, :]).astype(jnp.int32)
    earlier = jnp.cumsum(onehot, axis=0) - onehot
    position = jnp.sum(earlier * onehot, axis=1)
    slot = (flat_dest * capacity + position).reshape(rows_here, TOP)
    n_slots = n_ep * capacity
    matches = jnp.arange(n_slots, dtype=jnp.int32)[:, None, None] == slot[None]
    dispatch_table = jnp.any(matches, axis=-1).astype(jnp.bfloat16)
    outgoing = jnp.dot(dispatch_table, normed, preferred_element_type=jnp.float32).astype(
        jnp.bfloat16
    )
    outgoing = outgoing.reshape(n_ep, capacity, width)
    combine = jnp.transpose(
        jnp.sum(jnp.where(matches, gate_weights.astype(jnp.float32)[None], 0.0), axis=-1)
    ).astype(jnp.bfloat16)
    weight_in = expert_in[0]
    weight_out = expert_out[0]
    ff_here = weight_in.shape[2]
    weight_matrix = weight_in.reshape(width, 2 * ff_here)
    def expert(rows):
        both = jnp.dot(rows, weight_matrix, preferred_element_type=jnp.float32)
        hidden = (jax.nn.silu(both[:, :ff_here]) * both[:, ff_here:]).astype(jnp.bfloat16)
        return jnp.dot(hidden, weight_out, preferred_element_type=jnp.float32).astype(jnp.bfloat16)

    own = lax.all_to_all(outgoing, "ep", split_axis=0, concat_axis=0, tiled=True).reshape(
        n_slots, width
    )
    partial_own = expert(own)
    from_below, from_above = [None] * n_grp, [None] * n_grp
    up_rows, down_rows = own, own
    pending = []
    for r in range(1, n_grp):
        up_rows, down_rows = after(pending, up_rows), after(pending, down_rows)
        pending = [partial_own] if r == 1 else [from_below[r - 1], from_above[r - 1]]
        up_rows = shift_up(up_rows, r - 1, n_grp - 2)
        down_rows = shift_down(down_rows, 1, n_grp - r)
        if 2 * r <= n_grp - 1:
            pair = expert(jnp.concatenate([up_rows, down_rows], axis=0))
            from_below[r], from_above[r] = pair[:n_slots], pair[n_slots:]
        else:
            chosen = jnp.where(me_grp >= r, up_rows, down_rows)
            from_below[r] = from_above[r] = expert(chosen)
    up_sum = down_sum = None
    for r in range(1, n_grp):
        send_up = from_above[n_grp - r]
        send_down = from_below[n_grp - r]
        if r == 1:
            send_up, send_down = after(pending, send_up), after(pending, send_down)
        if r > 1:
            send_up = (send_up.astype(jnp.float32) + up_sum.astype(jnp.float32)).astype(
                jnp.bfloat16
            )
            send_down = (send_down.astype(jnp.float32) + down_sum.astype(jnp.float32)).astype(
                jnp.bfloat16
            )
        up_sum = shift_up(send_up, 0, r - 1)
        down_sum = shift_down(send_down, n_grp - r, n_grp - 1)
    expert_output = (
        partial_own.astype(jnp.float32) + up_sum.astype(jnp.float32) + down_sum.astype(jnp.float32)
    ).astype(jnp.bfloat16)
    summed = lax.all_to_all(
        expert_output.reshape(n_ep, capacity, width), "ep", split_axis=0, concat_axis=0, tiled=True
    ).reshape(n_slots, width)
    moe = jnp.dot(combine, summed, preferred_element_type=jnp.float32)
    return (residual + moe).astype(jnp.bfloat16)[None]


def solution(mesh):
    in_specs = (
        P("ep", "grp", None),
        P("ep", "grp", None),
        P("ep", "grp", None),
        P("ep", "grp", None),
        P("ep", "grp"),
        P(),
        P(),
        P(),
        P("ep", "grp", None),
        P("ep", None, None, "grp"),
        P("ep", "grp", None),
    )
    out_specs = P("ep", "grp", None)
    return jax.shard_map(local, mesh=mesh, in_specs=in_specs, out_specs=out_specs, check_vma=False)
```

```python
import jax
import jax.numpy as jnp
from jax import lax
from jax.sharding import PartitionSpec as P

HEADS = 36
HEAD_DIM = 64
EXPERTS = 8
TOP = 2


NEG = -1e30


def shift_up(x, first, last):
    return lax.ppermute(x, "grp", perm=[(i, i + 1) for i in range(first, last + 1)])


def shift_down(x, first, last):
    return lax.ppermute(x, "grp", perm=[(i, i - 1) for i in range(first, last + 1)])


def exchange(blocks, n_ep, sign):
    out = [blocks[0]]
    for k in range(1, n_ep):
        perm = [(i, (i + sign * k) % n_ep) for i in range(n_ep)]
        out.append(lax.ppermute(blocks[k], "ep", perm=perm))
    return jnp.stack(out)


def local(
    resid, queries, keys, values, tenant, out_proj, norm_gain, router, routes, expert_in, expert_out
):
    rows_here = resid.shape[1]
    width = resid.shape[2]
    n_ep = lax.axis_size("ep")
    n_grp = lax.axis_size("grp")
    seq_len = rows_here * n_grp
    replicas = n_ep // EXPERTS
    block = rows_here // replicas
    capacity = block * 5 // 16
    me_grp = lax.axis_index("grp")
    offset = me_grp * rows_here
    span = seq_len // 2
    back = min(n_grp - 1, -(-(span - 1) // rows_here))

    query_heads = queries[0].reshape(rows_here, HEADS, HEAD_DIM)
    query_pos = offset + jnp.arange(rows_here, dtype=jnp.int32)
    query_seg = tenant[0]
    scale = HEAD_DIM ** (-0.5)

    key_chunks = [keys[0]]
    value_chunks = [values[0]]
    seg_chunks = [tenant[0]]
    k_cur, v_cur, s_cur = keys[0], values[0], tenant[0]
    for _ in range(back):
        k_cur = shift_up(k_cur, 0, n_grp - 2)
        v_cur = shift_up(v_cur, 0, n_grp - 2)
        s_cur = shift_up(s_cur, 0, n_grp - 2)
        key_chunks.insert(0, k_cur)
        value_chunks.insert(0, v_cur)
        seg_chunks.insert(0, s_cur)
    key_piece = jnp.concatenate(key_chunks, axis=0)
    value_piece = jnp.concatenate(value_chunks, axis=0)
    seg_piece = jnp.concatenate(seg_chunks, axis=0)
    count = key_piece.shape[0]
    key_pos = offset - back * rows_here + jnp.arange(count, dtype=jnp.int32)
    key_heads = key_piece.reshape(count, HEADS, HEAD_DIM)
    value_heads = value_piece.reshape(count, HEADS, HEAD_DIM)
    scores = (
        jnp.einsum("qhd,khd->hqk", query_heads, key_heads, preferred_element_type=jnp.float32)
        * scale
    )
    allowed = (
        (query_pos[:, None] >= key_pos[None, :])
        & (key_pos[None, :] >= 0)
        & (query_seg[:, None] == seg_piece[None, :])
    )
    scores = jnp.where(allowed[None], scores, NEG)
    newest = jnp.max(scores, axis=-1)
    probs = jnp.where(allowed[None], jnp.exp(scores - newest[..., None]), 0.0)
    total = jnp.sum(probs, axis=-1)
    accum = jnp.einsum(
        "hqk,khd->hqd", probs.astype(jnp.bfloat16), value_heads, preferred_element_type=jnp.float32
    )
    attended = (
        jnp.transpose(accum / total[..., None], (1, 0, 2))
        .reshape(rows_here, width)
        .astype(jnp.bfloat16)
    )
    residual = resid[0].astype(jnp.float32) + jnp.dot(
        attended, out_proj, preferred_element_type=jnp.float32
    )
    normed = (
        residual
        * lax.rsqrt(jnp.mean(residual * residual, axis=-1, keepdims=True) + 1e-05)
        * norm_gain
    ).astype(jnp.bfloat16)
    logits = jnp.dot(normed, router, preferred_element_type=jnp.float32)
    local_routes = routes[0]
    expert_ids = jnp.arange(EXPERTS, dtype=jnp.int32)
    picked = jnp.sum(
        jnp.where(local_routes[:, :, None] == expert_ids[None, None, :], logits[:, None, :], 0.0),
        axis=-1,
    )
    gate_weights = jax.nn.softmax(picked, axis=-1).astype(jnp.bfloat16)
    half_id = jnp.arange(rows_here, dtype=jnp.int32) // block
    destination = local_routes * replicas + half_id[:, None]
    flat_dest = destination.reshape(-1)
    onehot = (flat_dest[:, None] == jnp.arange(n_ep, dtype=jnp.int32)[None, :]).astype(jnp.int32)
    earlier = jnp.cumsum(onehot, axis=0) - onehot
    position = jnp.sum(earlier * onehot, axis=1)
    slot = (flat_dest * capacity + position).reshape(rows_here, TOP)
    n_slots = n_ep * capacity
    matches = jnp.arange(n_slots, dtype=jnp.int32)[:, None, None] == slot[None]
    dispatch_table = jnp.any(matches, axis=-1).astype(jnp.bfloat16)
    outgoing = jnp.dot(dispatch_table, normed, preferred_element_type=jnp.float32).astype(
        jnp.bfloat16
    )
    outgoing = outgoing.reshape(n_ep, capacity, width)
    combine = jnp.transpose(
        jnp.sum(jnp.where(matches, gate_weights.astype(jnp.float32)[None], 0.0), axis=-1)
    ).astype(jnp.bfloat16)
    weight_in = expert_in[0]
    weight_out = expert_out[0]
    ff_here = weight_in.shape[2]
    weight_matrix = weight_in.reshape(width, 2 * ff_here)
    def expert(rows):
        both = jnp.dot(rows, weight_matrix, preferred_element_type=jnp.float32)
        hidden = (jax.nn.silu(both[:, :ff_here]) * both[:, ff_here:]).astype(jnp.bfloat16)
        return jnp.dot(hidden, weight_out, preferred_element_type=jnp.float32).astype(jnp.bfloat16)

    me_ep = lax.axis_index("ep")
    own = exchange(jnp.roll(outgoing, -me_ep, axis=0), n_ep, 1).reshape(n_slots, width)
    partial_own = expert(own)
    from_below, from_above = [None] * n_grp, [None] * n_grp
    up_rows, down_rows = own, own
    pending = []
    for r in range(1, n_grp):
        up_rows, down_rows, _ = lax.optimization_barrier((up_rows, down_rows, pending))
        pending = [partial_own] if r == 1 else [from_below[r - 1], from_above[r - 1]]
        up_rows = shift_up(up_rows, r - 1, n_grp - 2)
        down_rows = shift_down(down_rows, 1, n_grp - r)
        if 2 * r <= n_grp - 1:
            pair = expert(jnp.concatenate([up_rows, down_rows], axis=0))
            from_below[r], from_above[r] = pair[:n_slots], pair[n_slots:]
        else:
            chosen = jnp.where(me_grp >= r, up_rows, down_rows)
            from_below[r] = from_above[r] = expert(chosen)
    up_sum = down_sum = None
    for r in range(1, n_grp):
        send_up = from_above[n_grp - r]
        send_down = from_below[n_grp - r]
        if r == 1:
            send_up, send_down, _ = lax.optimization_barrier((send_up, send_down, pending))
        if r > 1:
            send_up = (send_up.astype(jnp.float32) + up_sum.astype(jnp.float32)).astype(
                jnp.bfloat16
            )
            send_down = (send_down.astype(jnp.float32) + down_sum.astype(jnp.float32)).astype(
                jnp.bfloat16
            )
        up_sum = shift_up(send_up, 0, r - 1)
        down_sum = shift_down(send_down, n_grp - r, n_grp - 1)
    expert_output = (
        partial_own.astype(jnp.float32) + up_sum.astype(jnp.float32) + down_sum.astype(jnp.float32)
    ).astype(jnp.bfloat16)
    back = exchange(expert_output.reshape(n_ep, capacity, width), n_ep, -1)
    summed = jnp.roll(back, me_ep, axis=0).reshape(n_slots, width)
    moe = jnp.dot(combine, summed, preferred_element_type=jnp.float32)
    return (residual + moe).astype(jnp.bfloat16)[None]


def solution(mesh):
    in_specs = (
        P("ep", "grp", None),
        P("ep", "grp", None),
        P("ep", "grp", None),
        P("ep", "grp", None),
        P("ep", "grp"),
        P(),
        P(),
        P(),
        P("ep", "grp", None),
        P("ep", None, None, "grp"),
        P("ep", "grp", None),
    )
    out_specs = P("ep", "grp", None)
    return jax.shard_map(local, mesh=mesh, in_specs=in_specs, out_specs=out_specs, check_vma=False)
```

```python
import jax
import jax.numpy as jnp
from jax import lax
from jax.sharding import PartitionSpec as P

HEADS = 36
HEAD_DIM = 64
EXPERTS = 8
TOP = 2


NEG = -1e30


def shift_up(x, first, last):
    return lax.ppermute(x, "grp", perm=[(i, i + 1) for i in range(first, last + 1)])


def shift_down(x, first, last):
    return lax.ppermute(x, "grp", perm=[(i, i - 1) for i in range(first, last + 1)])


def local(
    resid, queries, keys, values, tenant, out_proj, norm_gain, router, routes, expert_in, expert_out
):
    rows_here = resid.shape[1]
    width = resid.shape[2]
    n_ep = lax.axis_size("ep")
    n_grp = lax.axis_size("grp")
    seq_len = rows_here * n_grp
    replicas = n_ep // EXPERTS
    block = rows_here // replicas
    capacity = block * 5 // 16
    me_grp = lax.axis_index("grp")
    offset = me_grp * rows_here
    span = seq_len // 2
    back = min(n_grp - 1, -(-(span - 1) // rows_here))

    query_heads = queries[0].reshape(rows_here, HEADS, HEAD_DIM)
    query_pos = offset + jnp.arange(rows_here, dtype=jnp.int32)
    query_seg = tenant[0]
    scale = HEAD_DIM ** (-0.5)

    key_chunks = [keys[0]]
    value_chunks = [values[0]]
    seg_chunks = [tenant[0]]
    k_cur, v_cur, s_cur = keys[0], values[0], tenant[0]
    for _ in range(back):
        k_cur = shift_up(k_cur, 0, n_grp - 2)
        v_cur = shift_up(v_cur, 0, n_grp - 2)
        s_cur = shift_up(s_cur, 0, n_grp - 2)
        key_chunks.insert(0, k_cur)
        value_chunks.insert(0, v_cur)
        seg_chunks.insert(0, s_cur)
    key_piece = jnp.concatenate(key_chunks, axis=0)
    value_piece = jnp.concatenate(value_chunks, axis=0)
    seg_piece = jnp.concatenate(seg_chunks, axis=0)
    count = key_piece.shape[0]
    key_pos = offset - back * rows_here + jnp.arange(count, dtype=jnp.int32)
    key_heads = key_piece.reshape(count, HEADS, HEAD_DIM)
    value_heads = value_piece.reshape(count, HEADS, HEAD_DIM)
    scores = (
        jnp.einsum("qhd,khd->hqk", query_heads, key_heads, preferred_element_type=jnp.float32)
        * scale
    )
    allowed = (
        (query_pos[:, None] >= key_pos[None, :])
        & (key_pos[None, :] >= 0)
        & (query_seg[:, None] == seg_piece[None, :])
    )
    scores = jnp.where(allowed[None], scores, NEG)
    newest = jnp.max(scores, axis=-1)
    probs = jnp.where(allowed[None], jnp.exp(scores - newest[..., None]), 0.0)
    total = jnp.sum(probs, axis=-1)
    accum = jnp.einsum(
        "hqk,khd->hqd", probs.astype(jnp.bfloat16), value_heads, preferred_element_type=jnp.float32
    )
    attended = (
        jnp.transpose(accum / total[..., None], (1, 0, 2))
        .reshape(rows_here, width)
        .astype(jnp.bfloat16)
    )
    residual = resid[0].astype(jnp.float32) + jnp.dot(
        attended, out_proj, preferred_element_type=jnp.float32
    )
    normed = (
        residual
        * lax.rsqrt(jnp.mean(residual * residual, axis=-1, keepdims=True) + 1e-05)
        * norm_gain
    ).astype(jnp.bfloat16)
    logits = jnp.dot(normed, router, preferred_element_type=jnp.float32)
    local_routes = routes[0]
    expert_ids = jnp.arange(EXPERTS, dtype=jnp.int32)
    picked = jnp.sum(
        jnp.where(local_routes[:, :, None] == expert_ids[None, None, :], logits[:, None, :], 0.0),
        axis=-1,
    )
    gate_weights = jax.nn.softmax(picked, axis=-1).astype(jnp.bfloat16)
    half_id = jnp.arange(rows_here, dtype=jnp.int32) // block
    destination = local_routes * replicas + half_id[:, None]
    flat_dest = destination.reshape(-1)
    onehot = (flat_dest[:, None] == jnp.arange(n_ep, dtype=jnp.int32)[None, :]).astype(jnp.int32)
    earlier = jnp.cumsum(onehot, axis=0) - onehot
    position = jnp.sum(earlier * onehot, axis=1)
    slot = (flat_dest * capacity + position).reshape(rows_here, TOP)
    n_slots = n_ep * capacity
    matches = jnp.arange(n_slots, dtype=jnp.int32)[:, None, None] == slot[None]
    dispatch_table = jnp.any(matches, axis=-1).astype(jnp.bfloat16)
    outgoing = jnp.dot(dispatch_table, normed, preferred_element_type=jnp.float32).astype(
        jnp.bfloat16
    )
    outgoing = outgoing.reshape(n_ep, capacity, width)
    combine = jnp.transpose(
        jnp.sum(jnp.where(matches, gate_weights.astype(jnp.float32)[None], 0.0), axis=-1)
    ).astype(jnp.bfloat16)
    weight_in = expert_in[0]
    weight_out = expert_out[0]
    ff_here = weight_in.shape[2]
    weight_matrix = weight_in.reshape(width, 2 * ff_here)
    def expert(rows):
        both = jnp.dot(rows, weight_matrix, preferred_element_type=jnp.float32)
        hidden = (jax.nn.silu(both[:, :ff_here]) * both[:, ff_here:]).astype(jnp.bfloat16)
        return jnp.dot(hidden, weight_out, preferred_element_type=jnp.float32).astype(jnp.bfloat16)

    own = lax.all_to_all(outgoing, "ep", split_axis=0, concat_axis=0, tiled=True).reshape(
        n_slots, width
    )
    def grp_rounds(own):
        rows = own.shape[0]
        partial_own = expert(own)
        from_below, from_above = [None] * n_grp, [None] * n_grp
        up_rows, down_rows = own, own
        pending = []
        for r in range(1, n_grp):
            up_rows, down_rows, _ = lax.optimization_barrier((up_rows, down_rows, pending))
            pending = [partial_own] if r == 1 else [from_below[r - 1], from_above[r - 1]]
            up_rows = shift_up(up_rows, r - 1, n_grp - 2)
            down_rows = shift_down(down_rows, 1, n_grp - r)
            if 2 * r <= n_grp - 1:
                pair = expert(jnp.concatenate([up_rows, down_rows], axis=0))
                from_below[r], from_above[r] = pair[:rows], pair[rows:]
            else:
                chosen = jnp.where(me_grp >= r, up_rows, down_rows)
                from_below[r] = from_above[r] = expert(chosen)
        up_sum = down_sum = None
        for r in range(1, n_grp):
            send_up = from_above[n_grp - r]
            send_down = from_below[n_grp - r]
            if r == 1:
                send_up, send_down, _ = lax.optimization_barrier((send_up, send_down, pending))
            if r > 1:
                send_up = (send_up.astype(jnp.float32) + up_sum.astype(jnp.float32)).astype(
                    jnp.bfloat16
                )
                send_down = (send_down.astype(jnp.float32) + down_sum.astype(jnp.float32)).astype(
                    jnp.bfloat16
                )
            up_sum = shift_up(send_up, 0, r - 1)
            down_sum = shift_down(send_down, n_grp - r, n_grp - 1)
        expert_output = (
            partial_own.astype(jnp.float32) + up_sum.astype(jnp.float32) + down_sum.astype(jnp.float32)
        ).astype(jnp.bfloat16)

        return expert_output

    n_halves = 2 if capacity % 2 == 0 else 1
    part = capacity // n_halves
    own3 = own.reshape(n_ep, capacity, width)
    expert_output = jnp.concatenate(
        [
            grp_rounds(own3[:, h * part : (h + 1) * part].reshape(n_ep * part, width)).reshape(
                n_ep, part, width
            )
            for h in range(n_halves)
        ],
        axis=1,
    )
    summed = lax.all_to_all(
        expert_output.reshape(n_ep, capacity, width), "ep", split_axis=0, concat_axis=0, tiled=True
    ).reshape(n_slots, width)
    moe = jnp.dot(combine, summed, preferred_element_type=jnp.float32)
    return (residual + moe).astype(jnp.bfloat16)[None]


def solution(mesh):
    in_specs = (
        P("ep", "grp", None),
        P("ep", "grp", None),
        P("ep", "grp", None),
        P("ep", "grp", None),
        P("ep", "grp"),
        P(),
        P(),
        P(),
        P("ep", "grp", None),
        P("ep", None, None, "grp"),
        P("ep", "grp", None),
    )
    out_specs = P("ep", "grp", None)
    return jax.shard_map(local, mesh=mesh, in_specs=in_specs, out_specs=out_specs, check_vma=False)
```

```python
import jax
import jax.numpy as jnp
from jax import lax
from jax.sharding import PartitionSpec as P

HEADS = 36
HEAD_DIM = 64
EXPERTS = 8
TOP = 2


NEG = -1e30


def shift_up(x, first, last):
    return lax.ppermute(x, "grp", perm=[(i, i + 1) for i in range(first, last + 1)])


def shift_down(x, first, last):
    return lax.ppermute(x, "grp", perm=[(i, i - 1) for i in range(first, last + 1)])


def local(
    resid, queries, keys, values, tenant, out_proj, norm_gain, router, routes, expert_in, expert_out
):
    rows_here = resid.shape[1]
    width = resid.shape[2]
    n_ep = lax.axis_size("ep")
    n_grp = lax.axis_size("grp")
    seq_len = rows_here * n_grp
    replicas = n_ep // EXPERTS
    block = rows_here // replicas
    capacity = block * 5 // 16
    me_grp = lax.axis_index("grp")
    offset = me_grp * rows_here
    span = seq_len // 2
    back = min(n_grp - 1, -(-(span - 1) // rows_here))

    query_heads = queries[0].reshape(rows_here, HEADS, HEAD_DIM)
    query_pos = offset + jnp.arange(rows_here, dtype=jnp.int32)
    query_seg = tenant[0]
    scale = HEAD_DIM ** (-0.5)

    seg_cols = jnp.broadcast_to(tenant[0].astype(jnp.bfloat16)[:, None], (rows_here, 128))
    cur = jnp.concatenate([keys[0], values[0], seg_cols], axis=1)
    chunks = [cur]
    for _ in range(back):
        cur = shift_up(cur, 0, n_grp - 2)
        chunks.insert(0, cur)
    piece = jnp.concatenate(chunks, axis=0)
    key_piece = piece[:, :width]
    value_piece = piece[:, width : 2 * width]
    seg_piece = piece[:, 2 * width].astype(jnp.int32)
    count = key_piece.shape[0]
    key_pos = offset - back * rows_here + jnp.arange(count, dtype=jnp.int32)
    key_heads = key_piece.reshape(count, HEADS, HEAD_DIM)
    value_heads = value_piece.reshape(count, HEADS, HEAD_DIM)
    scores = (
        jnp.einsum("qhd,khd->hqk", query_heads, key_heads, preferred_element_type=jnp.float32)
        * scale
    )
    allowed = (
        (query_pos[:, None] >= key_pos[None, :])
        & (key_pos[None, :] >= 0)
        & (query_seg[:, None] == seg_piece[None, :])
    )
    scores = jnp.where(allowed[None], scores, NEG)
    newest = jnp.max(scores, axis=-1)
    probs = jnp.where(allowed[None], jnp.exp(scores - newest[..., None]), 0.0)
    total = jnp.sum(probs, axis=-1)
    accum = jnp.einsum(
        "hqk,khd->hqd", probs.astype(jnp.bfloat16), value_heads, preferred_element_type=jnp.float32
    )
    attended = (
        jnp.transpose(accum / total[..., None], (1, 0, 2))
        .reshape(rows_here, width)
        .astype(jnp.bfloat16)
    )
    residual = resid[0].astype(jnp.float32) + jnp.dot(
        attended, out_proj, preferred_element_type=jnp.float32
    )
    normed = (
        residual
        * lax.rsqrt(jnp.mean(residual * residual, axis=-1, keepdims=True) + 1e-05)
        * norm_gain
    ).astype(jnp.bfloat16)
    logits = jnp.dot(normed, router, preferred_element_type=jnp.float32)
    local_routes = routes[0]
    expert_ids = jnp.arange(EXPERTS, dtype=jnp.int32)
    picked = jnp.sum(
        jnp.where(local_routes[:, :, None] == expert_ids[None, None, :], logits[:, None, :], 0.0),
        axis=-1,
    )
    gate_weights = jax.nn.softmax(picked, axis=-1).astype(jnp.bfloat16)
    half_id = jnp.arange(rows_here, dtype=jnp.int32) // block
    destination = local_routes * replicas + half_id[:, None]
    flat_dest = destination.reshape(-1)
    onehot = (flat_dest[:, None] == jnp.arange(n_ep, dtype=jnp.int32)[None, :]).astype(jnp.int32)
    earlier = jnp.cumsum(onehot, axis=0) - onehot
    position = jnp.sum(earlier * onehot, axis=1)
    slot = (flat_dest * capacity + position).reshape(rows_here, TOP)
    n_slots = n_ep * capacity
    matches = jnp.arange(n_slots, dtype=jnp.int32)[:, None, None] == slot[None]
    dispatch_table = jnp.any(matches, axis=-1).astype(jnp.bfloat16)
    outgoing = jnp.dot(dispatch_table, normed, preferred_element_type=jnp.float32).astype(
        jnp.bfloat16
    )
    outgoing = outgoing.reshape(n_ep, capacity, width)
    combine = jnp.transpose(
        jnp.sum(jnp.where(matches, gate_weights.astype(jnp.float32)[None], 0.0), axis=-1)
    ).astype(jnp.bfloat16)
    weight_in = expert_in[0]
    weight_out = expert_out[0]
    ff_here = weight_in.shape[2]
    weight_matrix = weight_in.reshape(width, 2 * ff_here)
    def expert(rows):
        both = jnp.dot(rows, weight_matrix, preferred_element_type=jnp.float32)
        hidden = (jax.nn.silu(both[:, :ff_here]) * both[:, ff_here:]).astype(jnp.bfloat16)
        return jnp.dot(hidden, weight_out, preferred_element_type=jnp.float32).astype(jnp.bfloat16)

    own = lax.all_to_all(outgoing, "ep", split_axis=0, concat_axis=0, tiled=True).reshape(
        n_slots, width
    )
    partial_own = expert(own)
    from_below, from_above = [None] * n_grp, [None] * n_grp
    up_rows, down_rows = own, own
    pending = []
    for r in range(1, n_grp):
        up_rows, down_rows, _ = lax.optimization_barrier((up_rows, down_rows, pending))
        pending = [partial_own] if r == 1 else [from_below[r - 1], from_above[r - 1]]
        up_rows = shift_up(up_rows, r - 1, n_grp - 2)
        down_rows = shift_down(down_rows, 1, n_grp - r)
        if 2 * r <= n_grp - 1:
            pair = expert(jnp.concatenate([up_rows, down_rows], axis=0))
            from_below[r], from_above[r] = pair[:n_slots], pair[n_slots:]
        else:
            chosen = jnp.where(me_grp >= r, up_rows, down_rows)
            from_below[r] = from_above[r] = expert(chosen)
    up_sum = down_sum = None
    for r in range(1, n_grp):
        send_up = from_above[n_grp - r]
        send_down = from_below[n_grp - r]
        if r == 1:
            send_up, send_down, _ = lax.optimization_barrier((send_up, send_down, pending))
        if r > 1:
            send_up = (send_up.astype(jnp.float32) + up_sum.astype(jnp.float32)).astype(
                jnp.bfloat16
            )
            send_down = (send_down.astype(jnp.float32) + down_sum.astype(jnp.float32)).astype(
                jnp.bfloat16
            )
        up_sum = shift_up(send_up, 0, r - 1)
        down_sum = shift_down(send_down, n_grp - r, n_grp - 1)
    expert_output = (
        partial_own.astype(jnp.float32) + up_sum.astype(jnp.float32) + down_sum.astype(jnp.float32)
    ).astype(jnp.bfloat16)
    summed = lax.all_to_all(
        expert_output.reshape(n_ep, capacity, width), "ep", split_axis=0, concat_axis=0, tiled=True
    ).reshape(n_slots, width)
    moe = jnp.dot(combine, summed, preferred_element_type=jnp.float32)
    return (residual + moe).astype(jnp.bfloat16)[None]


def solution(mesh):
    in_specs = (
        P("ep", "grp", None),
        P("ep", "grp", None),
        P("ep", "grp", None),
        P("ep", "grp", None),
        P("ep", "grp"),
        P(),
        P(),
        P(),
        P("ep", "grp", None),
        P("ep", None, None, "grp"),
        P("ep", "grp", None),
    )
    out_specs = P("ep", "grp", None)
    return jax.shard_map(local, mesh=mesh, in_specs=in_specs, out_specs=out_specs, check_vma=False)
```

```python
import jax
import jax.numpy as jnp
from jax import lax
from jax.sharding import PartitionSpec as P

HEADS = 36
HEAD_DIM = 64
EXPERTS = 8
TOP = 2


NEG = -1e30


def shift_up(x, first, last):
    return lax.ppermute(x, "grp", perm=[(i, i + 1) for i in range(first, last + 1)])


def shift_down(x, first, last):
    return lax.ppermute(x, "grp", perm=[(i, i - 1) for i in range(first, last + 1)])


def local(
    resid, queries, keys, values, tenant, out_proj, norm_gain, router, routes, expert_in, expert_out
):
    rows_here = resid.shape[1]
    width = resid.shape[2]
    n_ep = lax.axis_size("ep")
    n_grp = lax.axis_size("grp")
    seq_len = rows_here * n_grp
    replicas = n_ep // EXPERTS
    block = rows_here // replicas
    capacity = block * 5 // 16
    me_grp = lax.axis_index("grp")
    offset = me_grp * rows_here
    span = seq_len // 2
    back = min(n_grp - 1, -(-(span - 1) // rows_here))

    query_heads = queries[0].reshape(rows_here, HEADS, HEAD_DIM)
    query_pos = offset + jnp.arange(rows_here, dtype=jnp.int32)
    query_seg = tenant[0]
    scale = HEAD_DIM ** (-0.5)

    key_chunks = [keys[0]]
    value_chunks = [values[0]]
    seg_chunks = [tenant[0]]
    k_cur, v_cur, s_cur = keys[0], values[0], tenant[0]
    for _ in range(back):
        k_cur = shift_up(k_cur, 0, n_grp - 2)
        v_cur = shift_up(v_cur, 0, n_grp - 2)
        s_cur = shift_up(s_cur, 0, n_grp - 2)
        key_chunks.insert(0, k_cur)
        value_chunks.insert(0, v_cur)
        seg_chunks.insert(0, s_cur)
    key_piece = jnp.concatenate(key_chunks, axis=0)
    value_piece = jnp.concatenate(value_chunks, axis=0)
    seg_piece = jnp.concatenate(seg_chunks, axis=0)
    count = key_piece.shape[0]
    key_pos = offset - back * rows_here + jnp.arange(count, dtype=jnp.int32)
    key_heads = key_piece.reshape(count, HEADS, HEAD_DIM)
    value_heads = value_piece.reshape(count, HEADS, HEAD_DIM)
    scores = (
        jnp.einsum("qhd,khd->hqk", query_heads, key_heads, preferred_element_type=jnp.float32)
        * scale
    )
    allowed = (
        (query_pos[:, None] >= key_pos[None, :])
        & (key_pos[None, :] >= 0)
        & (query_seg[:, None] == seg_piece[None, :])
    )
    scores = jnp.where(allowed[None], scores, NEG)
    newest = jnp.max(scores, axis=-1)
    probs = jnp.where(allowed[None], jnp.exp(scores - newest[..., None]), 0.0)
    total = jnp.sum(probs, axis=-1)
    accum = jnp.einsum(
        "hqk,khd->hqd", probs.astype(jnp.bfloat16), value_heads, preferred_element_type=jnp.float32
    )
    attended = (
        jnp.transpose(accum / total[..., None], (1, 0, 2))
        .reshape(rows_here, width)
        .astype(jnp.bfloat16)
    )
    residual = resid[0].astype(jnp.float32) + jnp.dot(
        attended, out_proj, preferred_element_type=jnp.float32
    )
    normed = (
        residual
        * lax.rsqrt(jnp.mean(residual * residual, axis=-1, keepdims=True) + 1e-05)
        * norm_gain
    ).astype(jnp.bfloat16)
    logits = jnp.dot(normed, router, preferred_element_type=jnp.float32)
    local_routes = routes[0]
    expert_ids = jnp.arange(EXPERTS, dtype=jnp.int32)
    picked = jnp.sum(
        jnp.where(local_routes[:, :, None] == expert_ids[None, None, :], logits[:, None, :], 0.0),
        axis=-1,
    )
    gate_weights = jax.nn.softmax(picked, axis=-1).astype(jnp.bfloat16)
    half_id = jnp.arange(rows_here, dtype=jnp.int32) // block
    destination = local_routes * replicas + half_id[:, None]
    flat_dest = destination.reshape(-1)
    onehot = (flat_dest[:, None] == jnp.arange(n_ep, dtype=jnp.int32)[None, :]).astype(jnp.int32)
    earlier = jnp.cumsum(onehot, axis=0) - onehot
    position = jnp.sum(earlier * onehot, axis=1)
    slot = (flat_dest * capacity + position).reshape(rows_here, TOP)
    n_slots = n_ep * capacity
    matches = jnp.arange(n_slots, dtype=jnp.int32)[:, None, None] == slot[None]
    dispatch_table = jnp.any(matches, axis=-1).astype(jnp.bfloat16)
    outgoing = jnp.dot(dispatch_table, normed, preferred_element_type=jnp.float32).astype(
        jnp.bfloat16
    )
    outgoing = outgoing.reshape(n_ep, capacity, width)
    combine = jnp.transpose(
        jnp.sum(jnp.where(matches, gate_weights.astype(jnp.float32)[None], 0.0), axis=-1)
    ).astype(jnp.bfloat16)
    weight_in = expert_in[0]
    weight_out = expert_out[0]
    ff_here = weight_in.shape[2]
    weight_matrix = weight_in.reshape(width, 2 * ff_here)
    def expert(rows):
        both = jnp.dot(rows, weight_matrix, preferred_element_type=jnp.float32)
        hidden = (jax.nn.silu(both[:, :ff_here]) * both[:, ff_here:]).astype(jnp.bfloat16)
        return jnp.dot(hidden, weight_out, preferred_element_type=jnp.float32).astype(jnp.bfloat16)

    own = lax.all_to_all(outgoing, "ep", split_axis=0, concat_axis=0, tiled=True).reshape(
        n_slots, width
    )
    partial_own = expert(own)
    from_below, from_above = [None] * n_grp, [None] * n_grp
    up_rows, down_rows = own, own
    pending = []
    for r in range(1, n_grp):
        up_rows, down_rows, _ = lax.optimization_barrier((up_rows, down_rows, pending))
        pending = [partial_own] if r == 1 else [from_below[r - 1], from_above[r - 1]]
        up_rows = shift_up(up_rows, r - 1, n_grp - 2)
        down_rows = shift_down(down_rows, 1, n_grp - r)
        if 2 * r <= n_grp - 1:
            pair = expert(jnp.concatenate([up_rows, down_rows], axis=0))
            from_below[r], from_above[r] = pair[:n_slots], pair[n_slots:]
        else:
            chosen = jnp.where(me_grp >= r, up_rows, down_rows)
            if r == n_grp - 1:
                half = n_slots // 2
                last_halves = [expert(chosen[:half]), expert(chosen[half:])]
            else:
                from_below[r] = from_above[r] = expert(chosen)
    up_sum = jnp.concatenate([shift_up(h, 0, 0) for h in last_halves], axis=0)
    down_sum = jnp.concatenate(
        [shift_down(h, n_grp - 1, n_grp - 1) for h in last_halves], axis=0
    )
    for r in range(2, n_grp):
        send_up = (from_above[n_grp - r].astype(jnp.float32) + up_sum.astype(jnp.float32)).astype(
            jnp.bfloat16
        )
        send_down = (
            from_below[n_grp - r].astype(jnp.float32) + down_sum.astype(jnp.float32)
        ).astype(jnp.bfloat16)
        up_sum = shift_up(send_up, 0, r - 1)
        down_sum = shift_down(send_down, n_grp - r, n_grp - 1)
    expert_output = (
        partial_own.astype(jnp.float32) + up_sum.astype(jnp.float32) + down_sum.astype(jnp.float32)
    ).astype(jnp.bfloat16)
    summed = lax.all_to_all(
        expert_output.reshape(n_ep, capacity, width), "ep", split_axis=0, concat_axis=0, tiled=True
    ).reshape(n_slots, width)
    moe = jnp.dot(combine, summed, preferred_element_type=jnp.float32)
    return (residual + moe).astype(jnp.bfloat16)[None]


def solution(mesh):
    in_specs = (
        P("ep", "grp", None),
        P("ep", "grp", None),
        P("ep", "grp", None),
        P("ep", "grp", None),
        P("ep", "grp"),
        P(),
        P(),
        P(),
        P("ep", "grp", None),
        P("ep", None, None, "grp"),
        P("ep", "grp", None),
    )
    out_specs = P("ep", "grp", None)
    return jax.shard_map(local, mesh=mesh, in_specs=in_specs, out_specs=out_specs, check_vma=False)
```

```python
import jax
import jax.numpy as jnp
from jax import lax
from jax.sharding import PartitionSpec as P

HEADS = 36
HEAD_DIM = 64
EXPERTS = 8
TOP = 2


NEG = -1e30


def shift_up(x, first, last):
    return lax.ppermute(x, "grp", perm=[(i, i + 1) for i in range(first, last + 1)])


def shift_down(x, first, last):
    return lax.ppermute(x, "grp", perm=[(i, i - 1) for i in range(first, last + 1)])


def local(
    resid, queries, keys, values, tenant, out_proj, norm_gain, router, routes, expert_in, expert_out
):
    rows_here = resid.shape[1]
    width = resid.shape[2]
    n_ep = lax.axis_size("ep")
    n_grp = lax.axis_size("grp")
    seq_len = rows_here * n_grp
    replicas = n_ep // EXPERTS
    block = rows_here // replicas
    capacity = block * 5 // 16
    me_grp = lax.axis_index("grp")
    offset = me_grp * rows_here
    span = seq_len // 2
    back = min(n_grp - 1, -(-(span - 1) // rows_here))

    query_heads = queries[0].reshape(rows_here, HEADS, HEAD_DIM)
    query_pos = offset + jnp.arange(rows_here, dtype=jnp.int32)
    query_seg = tenant[0]
    scale = HEAD_DIM ** (-0.5)

    seg_cols = jnp.broadcast_to(tenant[0].astype(jnp.bfloat16)[:, None], (rows_here, 128))
    k_cur = jnp.concatenate([keys[0], seg_cols], axis=1)
    v_cur = values[0]
    key_chunks, value_chunks = [k_cur], [v_cur]
    for _ in range(back):
        k_cur = shift_up(k_cur, 0, n_grp - 2)
        v_cur = shift_up(v_cur, 0, n_grp - 2)
        key_chunks.insert(0, k_cur)
        value_chunks.insert(0, v_cur)
    key_seg = jnp.concatenate(key_chunks, axis=0)
    key_piece = key_seg[:, :width]
    seg_piece = key_seg[:, width].astype(jnp.int32)
    value_piece = jnp.concatenate(value_chunks, axis=0)
    count = key_piece.shape[0]
    key_pos = offset - back * rows_here + jnp.arange(count, dtype=jnp.int32)
    key_heads = key_piece.reshape(count, HEADS, HEAD_DIM)
    value_heads = value_piece.reshape(count, HEADS, HEAD_DIM)
    scores = (
        jnp.einsum("qhd,khd->hqk", query_heads, key_heads, preferred_element_type=jnp.float32)
        * scale
    )
    allowed = (
        (query_pos[:, None] >= key_pos[None, :])
        & (key_pos[None, :] >= 0)
        & (query_seg[:, None] == seg_piece[None, :])
    )
    scores = jnp.where(allowed[None], scores, NEG)
    newest = jnp.max(scores, axis=-1)
    probs = jnp.where(allowed[None], jnp.exp(scores - newest[..., None]), 0.0)
    total = jnp.sum(probs, axis=-1)
    accum = jnp.einsum(
        "hqk,khd->hqd", probs.astype(jnp.bfloat16), value_heads, preferred_element_type=jnp.float32
    )
    attended = (
        jnp.transpose(accum / total[..., None], (1, 0, 2))
        .reshape(rows_here, width)
        .astype(jnp.bfloat16)
    )
    residual = resid[0].astype(jnp.float32) + jnp.dot(
        attended, out_proj, preferred_element_type=jnp.float32
    )
    normed = (
        residual
        * lax.rsqrt(jnp.mean(residual * residual, axis=-1, keepdims=True) + 1e-05)
        * norm_gain
    ).astype(jnp.bfloat16)
    logits = jnp.dot(normed, router, preferred_element_type=jnp.float32)
    local_routes = routes[0]
    expert_ids = jnp.arange(EXPERTS, dtype=jnp.int32)
    picked = jnp.sum(
        jnp.where(local_routes[:, :, None] == expert_ids[None, None, :], logits[:, None, :], 0.0),
        axis=-1,
    )
    gate_weights = jax.nn.softmax(picked, axis=-1).astype(jnp.bfloat16)
    half_id = jnp.arange(rows_here, dtype=jnp.int32) // block
    destination = local_routes * replicas + half_id[:, None]
    flat_dest = destination.reshape(-1)
    onehot = (flat_dest[:, None] == jnp.arange(n_ep, dtype=jnp.int32)[None, :]).astype(jnp.int32)
    earlier = jnp.cumsum(onehot, axis=0) - onehot
    position = jnp.sum(earlier * onehot, axis=1)
    slot = (flat_dest * capacity + position).reshape(rows_here, TOP)
    n_slots = n_ep * capacity
    matches = jnp.arange(n_slots, dtype=jnp.int32)[:, None, None] == slot[None]
    dispatch_table = jnp.any(matches, axis=-1).astype(jnp.bfloat16)
    outgoing = jnp.dot(dispatch_table, normed, preferred_element_type=jnp.float32).astype(
        jnp.bfloat16
    )
    outgoing = outgoing.reshape(n_ep, capacity, width)
    combine = jnp.transpose(
        jnp.sum(jnp.where(matches, gate_weights.astype(jnp.float32)[None], 0.0), axis=-1)
    ).astype(jnp.bfloat16)
    weight_in = expert_in[0]
    weight_out = expert_out[0]
    ff_here = weight_in.shape[2]
    weight_matrix = weight_in.reshape(width, 2 * ff_here)
    def expert(rows):
        both = jnp.dot(rows, weight_matrix, preferred_element_type=jnp.float32)
        hidden = (jax.nn.silu(both[:, :ff_here]) * both[:, ff_here:]).astype(jnp.bfloat16)
        return jnp.dot(hidden, weight_out, preferred_element_type=jnp.float32).astype(jnp.bfloat16)

    own = lax.all_to_all(outgoing, "ep", split_axis=0, concat_axis=0, tiled=True).reshape(
        n_slots, width
    )
    partial_own = expert(own)
    from_below, from_above = [None] * n_grp, [None] * n_grp
    up_rows, down_rows = own, own
    pending = []
    for r in range(1, n_grp):
        up_rows, down_rows, _ = lax.optimization_barrier((up_rows, down_rows, pending))
        pending = [partial_own] if r == 1 else [from_below[r - 1], from_above[r - 1]]
        up_rows = shift_up(up_rows, r - 1, n_grp - 2)
        down_rows = shift_down(down_rows, 1, n_grp - r)
        if 2 * r <= n_grp - 1:
            pair = expert(jnp.concatenate([up_rows, down_rows], axis=0))
            from_below[r], from_above[r] = pair[:n_slots], pair[n_slots:]
        else:
            chosen = jnp.where(me_grp >= r, up_rows, down_rows)
            from_below[r] = from_above[r] = expert(chosen)
    up_sum = down_sum = None
    for r in range(1, n_grp):
        send_up = from_above[n_grp - r]
        send_down = from_below[n_grp - r]
        if r == 1:
            send_up, send_down, _ = lax.optimization_barrier((send_up, send_down, pending))
        if r > 1:
            send_up = (send_up.astype(jnp.float32) + up_sum.astype(jnp.float32)).astype(
                jnp.bfloat16
            )
            send_down = (send_down.astype(jnp.float32) + down_sum.astype(jnp.float32)).astype(
                jnp.bfloat16
            )
        up_sum = shift_up(send_up, 0, r - 1)
        down_sum = shift_down(send_down, n_grp - r, n_grp - 1)
    expert_output = (
        partial_own.astype(jnp.float32) + up_sum.astype(jnp.float32) + down_sum.astype(jnp.float32)
    ).astype(jnp.bfloat16)
    summed = lax.all_to_all(
        expert_output.reshape(n_ep, capacity, width), "ep", split_axis=0, concat_axis=0, tiled=True
    ).reshape(n_slots, width)
    moe = jnp.dot(combine, summed, preferred_element_type=jnp.float32)
    return (residual + moe).astype(jnp.bfloat16)[None]


def solution(mesh):
    in_specs = (
        P("ep", "grp", None),
        P("ep", "grp", None),
        P("ep", "grp", None),
        P("ep", "grp", None),
        P("ep", "grp"),
        P(),
        P(),
        P(),
        P("ep", "grp", None),
        P("ep", None, None, "grp"),
        P("ep", "grp", None),
    )
    out_specs = P("ep", "grp", None)
    return jax.shard_map(local, mesh=mesh, in_specs=in_specs, out_specs=out_specs, check_vma=False)
```

```python
import jax
import jax.numpy as jnp
from jax import lax
from jax.sharding import PartitionSpec as P

HEADS = 36
HEAD_DIM = 64
EXPERTS = 8
TOP = 2


NEG = -1e30


def shift_up(x, first, last):
    return lax.ppermute(x, "grp", perm=[(i, i + 1) for i in range(first, last + 1)])


def shift_down(x, first, last):
    return lax.ppermute(x, "grp", perm=[(i, i - 1) for i in range(first, last + 1)])


def local(
    resid, queries, keys, values, tenant, out_proj, norm_gain, router, routes, expert_in, expert_out
):
    rows_here = resid.shape[1]
    width = resid.shape[2]
    n_ep = lax.axis_size("ep")
    n_grp = lax.axis_size("grp")
    seq_len = rows_here * n_grp
    replicas = n_ep // EXPERTS
    block = rows_here // replicas
    capacity = block * 5 // 16
    me_grp = lax.axis_index("grp")
    offset = me_grp * rows_here
    span = seq_len // 2
    back = min(n_grp - 1, -(-(span - 1) // rows_here))

    query_heads = queries[0].reshape(rows_here, HEADS, HEAD_DIM)
    query_pos = offset + jnp.arange(rows_here, dtype=jnp.int32)
    query_seg = tenant[0]
    scale = HEAD_DIM ** (-0.5)

    key_chunks = [keys[0]]
    value_chunks = [values[0]]
    seg_chunks = [tenant[0]]
    k_cur, v_cur, s_cur = keys[0], values[0], tenant[0]
    for _ in range(back):
        k_cur = shift_up(k_cur, 0, n_grp - 2)
        v_cur = shift_up(v_cur, 0, n_grp - 2)
        s_cur = shift_up(s_cur, 0, n_grp - 2)
        key_chunks.insert(0, k_cur)
        value_chunks.insert(0, v_cur)
        seg_chunks.insert(0, s_cur)
    scores, allowed = [], []
    for j in range(back + 1):
        key_pos = offset + (j - back) * rows_here + jnp.arange(rows_here, dtype=jnp.int32)
        key_heads = key_chunks[j].reshape(rows_here, HEADS, HEAD_DIM)
        kept = (
            (query_pos[:, None] >= key_pos[None, :])
            & (key_pos[None, :] >= 0)
            & (query_seg[:, None] == seg_chunks[j][None, :])
        )
        raw = (
            jnp.einsum("qhd,khd->hqk", query_heads, key_heads, preferred_element_type=jnp.float32)
            * scale
        )
        scores.append(jnp.where(kept[None], raw, NEG))
        allowed.append(kept)
    newest = scores[0].max(axis=-1)
    for part in scores[1:]:
        newest = jnp.maximum(newest, part.max(axis=-1))
    total = 0.0
    accum = 0.0
    for j in range(back + 1):
        probs = jnp.where(allowed[j][None], jnp.exp(scores[j] - newest[..., None]), 0.0)
        total = total + jnp.sum(probs, axis=-1)
        value_heads = value_chunks[j].reshape(rows_here, HEADS, HEAD_DIM)
        accum = accum + jnp.einsum(
            "hqk,khd->hqd",
            probs.astype(jnp.bfloat16),
            value_heads,
            preferred_element_type=jnp.float32,
        )
    attended = (
        jnp.transpose(accum / total[..., None], (1, 0, 2))
        .reshape(rows_here, width)
        .astype(jnp.bfloat16)
    )
    residual = resid[0].astype(jnp.float32) + jnp.dot(
        attended, out_proj, preferred_element_type=jnp.float32
    )
    normed = (
        residual
        * lax.rsqrt(jnp.mean(residual * residual, axis=-1, keepdims=True) + 1e-05)
        * norm_gain
    ).astype(jnp.bfloat16)
    logits = jnp.dot(normed, router, preferred_element_type=jnp.float32)
    local_routes = routes[0]
    expert_ids = jnp.arange(EXPERTS, dtype=jnp.int32)
    picked = jnp.sum(
        jnp.where(local_routes[:, :, None] == expert_ids[None, None, :], logits[:, None, :], 0.0),
        axis=-1,
    )
    gate_weights = jax.nn.softmax(picked, axis=-1).astype(jnp.bfloat16)
    half_id = jnp.arange(rows_here, dtype=jnp.int32) // block
    destination = local_routes * replicas + half_id[:, None]
    flat_dest = destination.reshape(-1)
    onehot = (flat_dest[:, None] == jnp.arange(n_ep, dtype=jnp.int32)[None, :]).astype(jnp.int32)
    earlier = jnp.cumsum(onehot, axis=0) - onehot
    position = jnp.sum(earlier * onehot, axis=1)
    slot = (flat_dest * capacity + position).reshape(rows_here, TOP)
    n_slots = n_ep * capacity
    matches = jnp.arange(n_slots, dtype=jnp.int32)[:, None, None] == slot[None]
    dispatch_table = jnp.any(matches, axis=-1).astype(jnp.bfloat16)
    outgoing = jnp.dot(dispatch_table, normed, preferred_element_type=jnp.float32).astype(
        jnp.bfloat16
    )
    outgoing = outgoing.reshape(n_ep, capacity, width)
    combine = jnp.transpose(
        jnp.sum(jnp.where(matches, gate_weights.astype(jnp.float32)[None], 0.0), axis=-1)
    ).astype(jnp.bfloat16)
    weight_in = expert_in[0]
    weight_out = expert_out[0]
    ff_here = weight_in.shape[2]
    weight_matrix = weight_in.reshape(width, 2 * ff_here)
    def expert(rows):
        both = jnp.dot(rows, weight_matrix, preferred_element_type=jnp.float32)
        hidden = (jax.nn.silu(both[:, :ff_here]) * both[:, ff_here:]).astype(jnp.bfloat16)
        return jnp.dot(hidden, weight_out, preferred_element_type=jnp.float32).astype(jnp.bfloat16)

    own = lax.all_to_all(outgoing, "ep", split_axis=0, concat_axis=0, tiled=True).reshape(
        n_slots, width
    )
    partial_own = expert(own)
    from_below, from_above = [None] * n_grp, [None] * n_grp
    up_rows, down_rows = own, own
    pending = []
    for r in range(1, n_grp):
        up_rows, down_rows, _ = lax.optimization_barrier((up_rows, down_rows, pending))
        pending = [partial_own] if r == 1 else [from_below[r - 1], from_above[r - 1]]
        up_rows = shift_up(up_rows, r - 1, n_grp - 2)
        down_rows = shift_down(down_rows, 1, n_grp - r)
        if 2 * r <= n_grp - 1:
            pair = expert(jnp.concatenate([up_rows, down_rows], axis=0))
            from_below[r], from_above[r] = pair[:n_slots], pair[n_slots:]
        else:
            chosen = jnp.where(me_grp >= r, up_rows, down_rows)
            from_below[r] = from_above[r] = expert(chosen)
    up_sum = down_sum = None
    for r in range(1, n_grp):
        send_up = from_above[n_grp - r]
        send_down = from_below[n_grp - r]
        if r == 1:
            send_up, send_down, _ = lax.optimization_barrier((send_up, send_down, pending))
        if r > 1:
            send_up = (send_up.astype(jnp.float32) + up_sum.astype(jnp.float32)).astype(
                jnp.bfloat16
            )
            send_down = (send_down.astype(jnp.float32) + down_sum.astype(jnp.float32)).astype(
                jnp.bfloat16
            )
        up_sum = shift_up(send_up, 0, r - 1)
        down_sum = shift_down(send_down, n_grp - r, n_grp - 1)
    expert_output = (
        partial_own.astype(jnp.float32) + up_sum.astype(jnp.float32) + down_sum.astype(jnp.float32)
    ).astype(jnp.bfloat16)
    summed = lax.all_to_all(
        expert_output.reshape(n_ep, capacity, width), "ep", split_axis=0, concat_axis=0, tiled=True
    ).reshape(n_slots, width)
    moe = jnp.dot(combine, summed, preferred_element_type=jnp.float32)
    return (residual + moe).astype(jnp.bfloat16)[None]


def solution(mesh):
    in_specs = (
        P("ep", "grp", None),
        P("ep", "grp", None),
        P("ep", "grp", None),
        P("ep", "grp", None),
        P("ep", "grp"),
        P(),
        P(),
        P(),
        P("ep", "grp", None),
        P("ep", None, None, "grp"),
        P("ep", "grp", None),
    )
    out_specs = P("ep", "grp", None)
    return jax.shard_map(local, mesh=mesh, in_specs=in_specs, out_specs=out_specs, check_vma=False)
```

```python
import jax
import jax.numpy as jnp
from jax import lax
from jax.sharding import PartitionSpec as P

HEADS = 36
HEAD_DIM = 64
EXPERTS = 8
TOP = 2


NEG = -1e30


def shift_up(x, first, last):
    return lax.ppermute(x, "grp", perm=[(i, i + 1) for i in range(first, last + 1)])


def shift_down(x, first, last):
    return lax.ppermute(x, "grp", perm=[(i, i - 1) for i in range(first, last + 1)])


def local(
    resid, queries, keys, values, tenant, out_proj, norm_gain, router, routes, expert_in, expert_out
):
    rows_here = resid.shape[1]
    width = resid.shape[2]
    n_ep = lax.axis_size("ep")
    n_grp = lax.axis_size("grp")
    seq_len = rows_here * n_grp
    replicas = n_ep // EXPERTS
    block = rows_here // replicas
    capacity = block * 5 // 16
    me_grp = lax.axis_index("grp")
    offset = me_grp * rows_here
    span = seq_len // 2
    back = min(n_grp - 1, -(-(span - 1) // rows_here))

    query_heads = queries[0].reshape(rows_here, HEADS, HEAD_DIM)
    query_pos = offset + jnp.arange(rows_here, dtype=jnp.int32)
    query_seg = tenant[0]
    scale = HEAD_DIM ** (-0.5)

    key_chunks = [keys[0]]
    value_chunks = [values[0]]
    seg_chunks = [tenant[0]]
    k_cur, v_cur, s_cur = keys[0], values[0], tenant[0]
    for _ in range(back):
        k_cur = shift_up(k_cur, 0, n_grp - 2)
        v_cur = shift_up(v_cur, 0, n_grp - 2)
        s_cur = shift_up(s_cur, 0, n_grp - 2)
        key_chunks.insert(0, k_cur)
        value_chunks.insert(0, v_cur)
        seg_chunks.insert(0, s_cur)
    scores, allowed = [], []
    for j in range(back + 1):
        key_pos = offset + (j - back) * rows_here + jnp.arange(rows_here, dtype=jnp.int32)
        key_heads = key_chunks[j].reshape(rows_here, HEADS, HEAD_DIM)
        kept = (
            (query_pos[:, None] >= key_pos[None, :])
            & (key_pos[None, :] >= 0)
            & (query_seg[:, None] == seg_chunks[j][None, :])
        )
        raw = (
            jnp.einsum("qhd,khd->hqk", query_heads, key_heads, preferred_element_type=jnp.float32)
            * scale
        )
        scores.append(jnp.where(kept[None], raw, NEG))
        allowed.append(kept)
    newest = scores[0].max(axis=-1)
    for part in scores[1:]:
        newest = jnp.maximum(newest, part.max(axis=-1))
    total = 0.0
    accum = 0.0
    for j in range(back + 1):
        probs = jnp.where(allowed[j][None], jnp.exp(scores[j] - newest[..., None]), 0.0)
        total = total + jnp.sum(probs, axis=-1)
        value_heads = value_chunks[j].reshape(rows_here, HEADS, HEAD_DIM)
        accum = accum + jnp.einsum(
            "hqk,khd->hqd",
            probs.astype(jnp.bfloat16),
            value_heads,
            preferred_element_type=jnp.float32,
        )
    attended = (
        jnp.transpose(accum / total[..., None], (1, 0, 2))
        .reshape(rows_here, width)
        .astype(jnp.bfloat16)
    )
    residual = resid[0].astype(jnp.float32) + jnp.dot(
        attended, out_proj, preferred_element_type=jnp.float32
    )
    normed = (
        residual
        * lax.rsqrt(jnp.mean(residual * residual, axis=-1, keepdims=True) + 1e-05)
        * norm_gain
    ).astype(jnp.bfloat16)
    logits = jnp.dot(normed, router, preferred_element_type=jnp.float32)
    local_routes = routes[0]
    expert_ids = jnp.arange(EXPERTS, dtype=jnp.int32)
    picked = jnp.sum(
        jnp.where(local_routes[:, :, None] == expert_ids[None, None, :], logits[:, None, :], 0.0),
        axis=-1,
    )
    gate_weights = jax.nn.softmax(picked, axis=-1).astype(jnp.bfloat16)
    half_id = jnp.arange(rows_here, dtype=jnp.int32) // block
    destination = local_routes * replicas + half_id[:, None]
    flat_dest = destination.reshape(-1)
    onehot = (flat_dest[:, None] == jnp.arange(n_ep, dtype=jnp.int32)[None, :]).astype(jnp.int32)
    earlier = jnp.cumsum(onehot, axis=0) - onehot
    position = jnp.sum(earlier * onehot, axis=1)
    slot = (flat_dest * capacity + position).reshape(rows_here, TOP)
    n_slots = n_ep * capacity
    matches = jnp.arange(n_slots, dtype=jnp.int32)[:, None, None] == slot[None]
    dispatch_table = jnp.any(matches, axis=-1).astype(jnp.bfloat16)
    outgoing = jnp.dot(dispatch_table, normed, preferred_element_type=jnp.float32).astype(
        jnp.bfloat16
    )
    outgoing = outgoing.reshape(n_ep, capacity, width)
    combine = jnp.transpose(
        jnp.sum(jnp.where(matches, gate_weights.astype(jnp.float32)[None], 0.0), axis=-1)
    ).astype(jnp.bfloat16)
    weight_in = expert_in[0]
    weight_out = expert_out[0]
    ff_here = weight_in.shape[2]
    weight_matrix = weight_in.reshape(width, 2 * ff_here)
    def expert(rows):
        both = jnp.dot(rows, weight_matrix, preferred_element_type=jnp.float32)
        hidden = (jax.nn.silu(both[:, :ff_here]) * both[:, ff_here:]).astype(jnp.bfloat16)
        return jnp.dot(hidden, weight_out, preferred_element_type=jnp.float32).astype(jnp.bfloat16)

    lanes = 128
    tiles = capacity * width // lanes
    own = lax.all_to_all(
        outgoing.reshape(n_ep, tiles, lanes), "ep", split_axis=0, concat_axis=0, tiled=True
    ).reshape(n_slots, width)
    partial_own = expert(own)
    from_below, from_above = [None] * n_grp, [None] * n_grp
    up_rows, down_rows = own, own
    pending = []
    for r in range(1, n_grp):
        up_rows, down_rows, _ = lax.optimization_barrier((up_rows, down_rows, pending))
        pending = [partial_own] if r == 1 else [from_below[r - 1], from_above[r - 1]]
        up_rows = shift_up(up_rows, r - 1, n_grp - 2)
        down_rows = shift_down(down_rows, 1, n_grp - r)
        if 2 * r <= n_grp - 1:
            pair = expert(jnp.concatenate([up_rows, down_rows], axis=0))
            from_below[r], from_above[r] = pair[:n_slots], pair[n_slots:]
        else:
            chosen = jnp.where(me_grp >= r, up_rows, down_rows)
            from_below[r] = from_above[r] = expert(chosen)
    up_sum = down_sum = None
    for r in range(1, n_grp):
        send_up = from_above[n_grp - r]
        send_down = from_below[n_grp - r]
        if r == 1:
            send_up, send_down, _ = lax.optimization_barrier((send_up, send_down, pending))
        if r > 1:
            send_up = (send_up.astype(jnp.float32) + up_sum.astype(jnp.float32)).astype(
                jnp.bfloat16
            )
            send_down = (send_down.astype(jnp.float32) + down_sum.astype(jnp.float32)).astype(
                jnp.bfloat16
            )
        up_sum = shift_up(send_up, 0, r - 1)
        down_sum = shift_down(send_down, n_grp - r, n_grp - 1)
    expert_output = (
        partial_own.astype(jnp.float32) + up_sum.astype(jnp.float32) + down_sum.astype(jnp.float32)
    ).astype(jnp.bfloat16)
    summed = lax.all_to_all(
        expert_output.reshape(n_ep, tiles, lanes), "ep", split_axis=0, concat_axis=0, tiled=True
    ).reshape(n_slots, width)
    moe = jnp.dot(combine, summed, preferred_element_type=jnp.float32)
    return (residual + moe).astype(jnp.bfloat16)[None]


def solution(mesh):
    in_specs = (
        P("ep", "grp", None),
        P("ep", "grp", None),
        P("ep", "grp", None),
        P("ep", "grp", None),
        P("ep", "grp"),
        P(),
        P(),
        P(),
        P("ep", "grp", None),
        P("ep", None, None, "grp"),
        P("ep", "grp", None),
    )
    out_specs = P("ep", "grp", None)
    return jax.shard_map(local, mesh=mesh, in_specs=in_specs, out_specs=out_specs, check_vma=False)
```
